512 devices in a mesh: expert: 64 (over y, z_hi, core), narrow: 8 (over z_lo, x).
Axes of the slice: x: 4, y: 8, z: 8 (z_hi: 4, z_lo: 2; z = z_hi * 2 + z_lo), core: 2. Of those that a mesh axis runs over, the one named last changes fastest.
Arguments:
- tokens: bfloat16 [3072, 4096], P('expert', 'narrow'), may hold values from -6 to 6
- route_ids: int32 [3072, 8], P('expert'), may hold values from 0 to 63, all different within a row; in each aligned block of 48 rows (0 to 47, 48 to 95, ...) at most 12 rows name the same one
- route_weight: bfloat16 [3072, 8], P('expert'), may hold values from 0.049804688 to 0.5
- partner: int32 [64], replicated, may hold values from 0 to 63, as said below
- old_place: int32 [64], replicated, may hold values from 0 to 63, each once
- gate_weight: bfloat16 [64, 768, 4096], P('expert', 'narrow'), may hold values from -0.09375 to 0.09375
- up_weight: bfloat16 [64, 768, 4096], P('expert', 'narrow'), may hold values from -0.09375 to 0.09375
- down_weight: bfloat16 [64, 768, 4096], P('expert', None, 'narrow'), may hold values from -0.21875 to 0.21875
Outputs:
- layer_out: bfloat16 [3072, 4096], P('expert', 'narrow')
- new_gate: bfloat16 [64, 768, 4096], P('expert', 'narrow')
- new_up: bfloat16 [64, 768, 4096], P('expert', 'narrow')
- new_down: bfloat16 [64, 768, 4096], P('expert', None, 'narrow')
The draws below stay inside these ranges and needn't reach their ends.
Inputs may be any that keep to these rules, and one draw needn't show every extreme that they name: partner[partner[s]] == s for every slot; slots with partner[s] == s keep their weights; the number of pairs varies between draws from 1 to 32. `old_place`: a permutation of the experts. `route_ids`: each row names 8 different experts; among the 48 tokens of one index of expert, no expert is named by more than 12 tokens.
All inputs are finite; a program needn't handle non-finite values.
Results may differ from the reference program's by a relative error of at most 0.0058.
Values may be sent and summed in bfloat16 or wider, within the bound.
No kernel may reach another device: no remote copies, remote signals or barrier semaphores. Data moves between devices by JAX's collectives and lax.ppermute only.
A program may use at most 128 MiB of HBM per device.

```python
import math
import jax
import jax.numpy as jnp
import numpy as np
from jax import lax

D = 4096
HID = 768
TOP = 8
TOK_GRP = 48
EXPERTS = 64
TOKENS = 3072
CAP = 12
ROWS = 768


def draw_partner(key, part):
    order = jax.random.permutation(jax.random.fold_in(key, 11), EXPERTS).astype(jnp.int32)
    pairs = jax.random.randint(jax.random.fold_in(key, 12), (), 1, EXPERTS // 2 + 1)
    position = jnp.arange(EXPERTS, dtype=jnp.int32)
    mate = jnp.where(position < 2 * pairs, position + 1 - 2 * (position % 2), position)
    return jnp.zeros((EXPERTS,), jnp.int32).at[order].set(order[mate]).astype(jnp.int32)


def shard_levels(stream_key, extent, split, smallest, largest):
    gain = 1.0
    for axis_at, parts in split:
        heights = jax.random.uniform(jax.random.fold_in(jax.random.fold_in(stream_key, 6), axis_at), (parts,), jnp.float32, smallest / len(split), largest / len(split))
        gain = gain * jnp.repeat(jnp.exp(heights), extent[axis_at] // parts).reshape((-1,) + (1,) * (len(extent) - 1 - axis_at))
    return gain


def deal_out(stream_key, own, number, rows, amount, top, limit, lean):
    order = jax.random.permutation(stream_key, amount)
    crowded, common = load_shares(amount, rows * top, limit, lean, True), load_shares(amount, rows * top, limit, lean, False)
    places = jnp.arange(amount)

    def named(sizes, offset_by):
        used = int((sizes > 0).sum())
        fixed = max(1, used // 4)
        passed = fixed + (places - fixed + offset_by * (used - fixed)) % max(1, amount - fixed)
        return jnp.zeros((amount,), jnp.int32).at[order[jnp.where(places < fixed, places, passed)]].set(jnp.asarray(sizes, jnp.int32))

    sizes = jnp.where(number % 4 == 0, named(crowded, number // 4), named(common, number - number // 4 - 1))
    mixed = jax.random.permutation(jax.random.fold_in(own, 3), amount)
    giver, taker = mixed[0:amount // 2 * 2:2], mixed[1:amount // 2 * 2:2]
    room = jnp.minimum(sizes[giver] - 1, limit - sizes[taker]) // 2
    room = jnp.where((giver == order[0]) | (taker == order[0]) | (sizes[taker] == 0), 0, jnp.maximum(room, 0))
    passed = jax.random.randint(jax.random.fold_in(own, 4), (amount // 2,), 0, 1 << 20) % (room + 1)
    sizes = sizes.at[giver].add(-passed).at[taker].add(passed)
    labels = jnp.searchsorted(jnp.cumsum(sizes), jnp.arange(rows * top), side="right").astype(jnp.int32)
    table = labels.reshape(top, rows).T
    table = table[jax.random.permutation(jax.random.fold_in(own, 1), rows)]
    offset_by = jax.random.randint(jax.random.fold_in(own, 2), (rows, 1), 0, top)
    return jnp.take_along_axis(table, (jnp.arange(top)[None, :] + offset_by) % top, axis=1)


def load_shares(number_of, total, limit, slope, full):
    weights = [(1 << 20) // math.isqrt(standing ** slope) + 1 for standing in range(1, number_of + 1)]
    largest = limit if full else min(limit, max(-(-total // number_of), total * weights[0] // sum(weights)))
    least = 1 if total - largest >= number_of - 1 else 0
    counts, rest = [largest] + [least] * (number_of - 1), total - largest - least * (number_of - 1)
    while rest > 0:
        free = [i for i in range(1, number_of) if counts[i] < largest] or [i for i in range(1, number_of) if counts[i] < limit]
        pool, budget = sum([weights[i] for i in free]), rest
        for i in free:
            extra = min(limit - counts[i], max(1, budget * weights[i] // pool), rest)
            counts[i] = counts[i] + extra
            rest = rest - extra
    return np.array(counts)


def centred(stream_key, extent, scale, limit, shards=(), kind=jnp.bfloat16):
    gain = shard_levels(stream_key, extent, shards, -0.22, 0.18) if shards else 1.0
    result = jax.random.normal(stream_key, extent, jnp.float32) * scale * gain
    return jnp.minimum(jnp.maximum(result, -limit), limit).astype(kind)


def setup_inputs(seed: int = 0) -> dict:
    seeds = jax.random.split(jax.random.key(seed), 9)
    tokens = centred(seeds[0], (TOKENS, D), 1.0, 6.0, ((0, 64), (1, 8)))
    route_ids_keys = jax.random.split(jax.random.fold_in(seeds[1], 1), TOKENS // TOK_GRP)
    route_ids_turns = jax.random.permutation(jax.random.fold_in(seeds[1], 3), TOKENS // TOK_GRP)
    route_ids = jax.vmap(lambda own, number: deal_out(jax.random.fold_in(seeds[1], 2), own, number, TOK_GRP, EXPERTS, TOP, CAP, 2))(route_ids_keys, route_ids_turns).reshape((TOKENS, TOP))
    route_weight = jnp.clip(0.049804688 + 0.4501953 * jax.random.uniform(seeds[2], (TOKENS, TOP), jnp.float32) ** shard_levels(seeds[2], (TOKENS, TOP), ((0, 64),), -0.2, 0.2), 0.049804688, 0.5).astype(jnp.bfloat16)
    partner = draw_partner(jax.random.fold_in(seeds[8], 71), 0)
    old_place = jax.random.permutation(seeds[4], EXPERTS).astype(jnp.int32)
    gate_weight = centred(seeds[5], (EXPERTS, HID, D), D ** -0.5, 0.09375, ((0, 64), (1, 8)))
    up_weight = centred(seeds[6], (EXPERTS, HID, D), D ** -0.5, 0.09375, ((0, 64), (1, 8)))
    down_weight = centred(seeds[7], (EXPERTS, HID, D), HID ** -0.5, 0.21875, ((0, 64), (2, 8)))
    return dict(tokens=tokens, route_ids=route_ids, route_weight=route_weight, partner=partner, old_place=old_place, gate_weight=gate_weight, up_weight=up_weight, down_weight=down_weight)


def expert_block(rows_in, gate_slot, up_slot, down_slot):
    gate_sum = lax.dot_general(rows_in, gate_slot, (((1,), (1,)), ((), ())), preferred_element_type=jnp.float32)
    up_sum = lax.dot_general(rows_in, up_slot, (((1,), (1,)), ((), ())), preferred_element_type=jnp.float32)
    hidden = (jax.nn.silu(gate_sum) * up_sum).astype(jnp.bfloat16)
    return jnp.dot(hidden, down_slot, preferred_element_type=jnp.float32).astype(jnp.bfloat16)


def reference(tokens, route_ids, route_weight, partner, old_place, gate_weight, up_weight, down_weight):
    weights_full = route_weight.astype(jnp.float32)

    def per_slot(totals, inputs):
        gate_slot, up_slot, down_slot, expert_id = inputs
        chosen_mask = route_ids == expert_id
        chosen = jnp.any(chosen_mask, axis=1)
        share = jnp.sum(jnp.where(chosen_mask, weights_full, jnp.zeros_like(weights_full)), axis=1)
        position = (jnp.cumsum(chosen.astype(jnp.int32)) - 1).astype(jnp.int32)
        target = jnp.where(chosen, position, ROWS).astype(jnp.int32)
        buffer_rows = jnp.zeros((ROWS, D), jnp.bfloat16).at[target].set(tokens, mode="drop")
        produced = expert_block(buffer_rows, gate_slot, up_slot, down_slot)
        picked = jnp.take(produced, jnp.clip(position, 0, ROWS - 1).astype(jnp.int32), axis=0)
        return totals + share[:, None] * picked.astype(jnp.float32), None

    start_totals = jnp.zeros((TOKENS, D), jnp.float32)
    totals = lax.scan(per_slot, start_totals, (gate_weight, up_weight, down_weight, old_place))[0]
    new_gate = jnp.take(gate_weight, partner, axis=0)
    new_up = jnp.take(up_weight, partner, axis=0)
    new_down = jnp.take(down_weight, partner, axis=0)
    return (totals.astype(jnp.bfloat16), new_gate, new_up, new_down)
```

```python
import jax
import jax.numpy as jnp
from jax import lax
from jax.sharding import PartitionSpec as P

LANES = 128


def slot_layout(route_ids, route_weight, holder, groups):
    tokens_here, top_count = route_ids.shape
    capacity = 2 * tokens_here * top_count // groups
    slot_ids = jnp.arange(groups, dtype=jnp.int32)
    matches = (holder[None, None, :] == route_ids[:, :, None]).astype(jnp.int32)
    target = jnp.sum(matches * slot_ids[None, None, :], axis=2)
    onehot = matches.reshape(tokens_here * top_count, groups)
    running = jnp.cumsum(onehot, axis=0) - 1
    position = jnp.sum(onehot * running, axis=1).reshape(tokens_here, top_count)
    row_index = target * capacity + position
    buffer_rows = jnp.arange(groups * capacity, dtype=jnp.int32)
    row_hits = buffer_rows[:, None, None] == row_index[None, :, :]
    dispatch = jnp.sum(row_hits.astype(jnp.float32), axis=2).astype(jnp.bfloat16)
    token_hits = row_index[:, :, None] == buffer_rows[None, None, :]
    combine = jnp.sum(
        jnp.where(token_hits, route_weight[:, :, None], jnp.zeros((), jnp.bfloat16)), axis=1
    )
    return (dispatch, combine, capacity)


def contract_last(left, right):
    return lax.dot_general(
        left, right, (((1,), (1,)), ((), ())), preferred_element_type=jnp.float32
    )


def pack_weights(gate, up, down, groups):
    rows, width = gate.shape
    depth, narrow_width = down.shape
    gate_c = gate.reshape(rows, width // LANES, LANES).transpose(1, 0, 2)
    up_c = up.reshape(rows, width // LANES, LANES).transpose(1, 0, 2)
    down_c = (
        down.reshape(depth // rows, rows, narrow_width // LANES, LANES)
        .transpose(0, 2, 1, 3)
        .reshape(-1, rows, LANES)
    )
    stacked = jnp.concatenate([gate_c, up_c, down_c], axis=0)
    return stacked.reshape(groups, -1, LANES)


def unpack_weights(packed, gate_shape, down_shape):
    rows, width = gate_shape
    depth, narrow_width = down_shape
    chunks = packed.reshape(-1, rows, LANES)
    n_gate = width // LANES
    gate = chunks[:n_gate].transpose(1, 0, 2).reshape(rows, width)
    up = chunks[n_gate : 2 * n_gate].transpose(1, 0, 2).reshape(rows, width)
    down = (
        chunks[2 * n_gate :]
        .reshape(depth // rows, narrow_width // LANES, rows, LANES)
        .transpose(0, 2, 1, 3)
        .reshape(depth, narrow_width)
    )
    return gate, up, down


def exchange(gate, up, down, partner, groups):
    packed = pack_weights(gate, up, down, groups)
    spread = lax.all_to_all(packed, "expert", split_axis=0, concat_axis=0, tiled=True)
    ordered = jnp.take(spread, partner, axis=0)
    arrived = lax.all_to_all(ordered, "expert", split_axis=0, concat_axis=0, tiled=True)
    return unpack_weights(arrived, gate.shape, down.shape)


def body(tokens, route_ids, route_weight, partner, old_place, gate_weight, up_weight, down_weight):
    groups = lax.axis_size("expert")
    gate_block = gate_weight[0]
    up_block = up_weight[0]
    down_block = down_weight[0]

    new_gate, new_up, new_down = exchange(gate_block, up_block, down_block, partner, groups)

    dispatch, combine, capacity = slot_layout(route_ids, route_weight, old_place, groups)
    outgoing = jnp.dot(dispatch, tokens, preferred_element_type=jnp.float32).astype(jnp.bfloat16)
    arrived_rows = lax.all_to_all(
        outgoing.reshape(groups, capacity, -1), "expert", split_axis=0, concat_axis=0, tiled=True
    )
    slice_rows = arrived_rows.reshape(-1, arrived_rows.shape[2])
    flat_rows = lax.all_gather(slice_rows, "narrow", axis=1, tiled=True)
    gate_sum = contract_last(flat_rows, gate_block)
    up_sum = contract_last(flat_rows, up_block)
    hidden = (jax.nn.silu(gate_sum) * up_sum).astype(jnp.bfloat16)
    produced = (
        jnp.dot(
            lax.all_gather(hidden, "narrow", axis=1, tiled=True),
            down_block,
            preferred_element_type=jnp.float32,
        )
        .astype(jnp.bfloat16)
        .reshape(groups, capacity, -1)
    )
    returned = lax.all_to_all(produced, "expert", split_axis=0, concat_axis=0, tiled=True)
    layer_out = jnp.dot(
        combine, returned.reshape(-1, returned.shape[2]), preferred_element_type=jnp.float32
    ).astype(jnp.bfloat16)
    return (
        layer_out,
        new_gate.reshape(gate_weight.shape),
        new_up.reshape(up_weight.shape),
        new_down.reshape(down_weight.shape),
    )


def solution(mesh):
    return jax.shard_map(
        body,
        mesh=mesh,
        in_specs=(
            P("expert", "narrow"),
            P("expert", None),
            P("expert", None),
            P(),
            P(),
            P("expert", "narrow", None),
            P("expert", "narrow", None),
            P("expert", None, "narrow"),
        ),
        out_specs=(
            P("expert", "narrow"),
            P("expert", "narrow", None),
            P("expert", "narrow", None),
            P("expert", None, "narrow"),
        ),
        check_vma=False,
    )
```

```python
import jax
import jax.numpy as jnp
from jax import lax
from jax.sharding import Mesh, PartitionSpec as P

LANES = 128


def slot_layout(route_ids, route_weight, holder, groups):
    tokens_here, top_count = route_ids.shape
    capacity = 2 * tokens_here * top_count // groups
    slot_ids = jnp.arange(groups, dtype=jnp.int32)
    matches = (holder[None, None, :] == route_ids[:, :, None]).astype(jnp.int32)
    target = jnp.sum(matches * slot_ids[None, None, :], axis=2)
    onehot = matches.reshape(tokens_here * top_count, groups)
    running = jnp.cumsum(onehot, axis=0) - 1
    position = jnp.sum(onehot * running, axis=1).reshape(tokens_here, top_count)
    row_index = target * capacity + position
    buffer_rows = jnp.arange(groups * capacity, dtype=jnp.int32)
    row_hits = buffer_rows[:, None, None] == row_index[None, :, :]
    dispatch = jnp.sum(row_hits.astype(jnp.float32), axis=2).astype(jnp.bfloat16)
    token_hits = row_index[:, :, None] == buffer_rows[None, None, :]
    combine = jnp.sum(
        jnp.where(token_hits, route_weight[:, :, None], jnp.zeros((), jnp.bfloat16)), axis=1
    )
    return (dispatch, combine, capacity)


def contract_last(left, right):
    return lax.dot_general(
        left, right, (((1,), (1,)), ((), ())), preferred_element_type=jnp.float32
    )


def pack_weights(gate, up, down, groups):
    rows, width = gate.shape
    depth, narrow_width = down.shape
    gate_c = gate.reshape(rows, width // LANES, LANES).transpose(1, 0, 2)
    up_c = up.reshape(rows, width // LANES, LANES).transpose(1, 0, 2)
    down_c = (
        down.reshape(depth // rows, rows, narrow_width // LANES, LANES)
        .transpose(0, 2, 1, 3)
        .reshape(-1, rows, LANES)
    )
    stacked = jnp.concatenate([gate_c, up_c, down_c], axis=0)
    return stacked.reshape(groups, -1, LANES)


def unpack_weights(packed, gate_shape, down_shape):
    rows, width = gate_shape
    depth, narrow_width = down_shape
    chunks = packed.reshape(-1, rows, LANES)
    n_gate = width // LANES
    gate = chunks[:n_gate].transpose(1, 0, 2).reshape(rows, width)
    up = chunks[n_gate : 2 * n_gate].transpose(1, 0, 2).reshape(rows, width)
    down = (
        chunks[2 * n_gate :]
        .reshape(depth // rows, narrow_width // LANES, rows, LANES)
        .transpose(0, 2, 1, 3)
        .reshape(depth, narrow_width)
    )
    return gate, up, down


def exchange(gate, up, down, partner, groups):
    packed = pack_weights(gate, up, down, groups)
    spread = lax.all_to_all(packed, "expert", split_axis=0, concat_axis=0, tiled=True)
    ordered = jnp.take(spread, partner, axis=0)
    arrived = lax.all_to_all(ordered, "expert", split_axis=0, concat_axis=0, tiled=True)
    return unpack_weights(arrived, gate.shape, down.shape)


def body(tokens, route_ids, route_weight, partner, old_place, gate_weight, up_weight, down_weight):
    groups = lax.axis_size("expert")
    half = lax.axis_index("zlo")
    gate_block = gate_weight[0]
    up_block = up_weight[0]
    down_block = down_weight[0]

    new_gate, new_up, new_down = exchange(gate_block, up_block, down_block, partner, groups)

    rows, width = gate_block.shape
    pair = [(0, 1), (1, 0)]
    gate_halves = gate_block.reshape(rows, 2, width // 2)
    up_halves = up_block.reshape(rows, 2, width // 2)
    keep = jnp.concatenate(
        [jnp.take(gate_halves, half, axis=1), jnp.take(up_halves, half, axis=1)], axis=0
    )
    give = jnp.concatenate(
        [jnp.take(gate_halves, 1 - half, axis=1), jnp.take(up_halves, 1 - half, axis=1)], axis=0
    )
    taken = lax.ppermute(give, "zlo", pair)

    dispatch, combine, capacity = slot_layout(route_ids, route_weight, old_place, groups)
    outgoing = jnp.dot(dispatch, tokens, preferred_element_type=jnp.float32).astype(jnp.bfloat16)
    arrived_rows = lax.all_to_all(
        outgoing.reshape(groups, capacity, -1), "expert", split_axis=0, concat_axis=0, tiled=True
    )
    slice_rows = arrived_rows.reshape(-1, arrived_rows.shape[2])
    half_rows = lax.all_gather(slice_rows, "x", axis=1, tiled=True)
    own_part = contract_last(half_rows, keep)
    other_part = contract_last(half_rows, taken)
    back = lax.ppermute(other_part, "zlo", pair)
    sums = own_part + back
    gate_sum = sums[:, :rows]
    up_sum = sums[:, rows:]
    hidden = (jax.nn.silu(gate_sum) * up_sum).astype(jnp.bfloat16)
    produced = (
        jnp.dot(
            lax.all_gather(hidden, ("zlo", "x"), axis=1, tiled=True),
            down_block,
            preferred_element_type=jnp.float32,
        )
        .astype(jnp.bfloat16)
        .reshape(groups, capacity, -1)
    )
    returned = lax.all_to_all(produced, "expert", split_axis=0, concat_axis=0, tiled=True)
    layer_out = jnp.dot(
        combine, returned.reshape(-1, returned.shape[2]), preferred_element_type=jnp.float32
    ).astype(jnp.bfloat16)
    return (
        layer_out,
        new_gate.reshape(gate_weight.shape),
        new_up.reshape(up_weight.shape),
        new_down.reshape(down_weight.shape),
    )


def solution(mesh):
    expert_size, narrow_size = mesh.devices.shape
    split_mesh = Mesh(
        mesh.devices.reshape(expert_size, 2, narrow_size // 2), ("expert", "zlo", "x")
    )
    narrow = ("zlo", "x")
    return jax.shard_map(
        body,
        mesh=split_mesh,
        in_specs=(
            P("expert", narrow),
            P("expert", None),
            P("expert", None),
            P(),
            P(),
            P("expert", narrow, None),
            P("expert", narrow, None),
            P("expert", None, narrow),
        ),
        out_specs=(
            P("expert", narrow),
            P("expert", narrow, None),
            P("expert", narrow, None),
            P("expert", None, narrow),
        ),
        check_vma=False,
    )
```

```python
import jax
import jax.numpy as jnp
from jax import lax
from jax.sharding import Mesh, PartitionSpec as P

LANES = 128


def slot_layout(route_ids, route_weight, holder, groups):
    tokens_here, top_count = route_ids.shape
    capacity = 2 * tokens_here * top_count // groups
    slot_ids = jnp.arange(groups, dtype=jnp.int32)
    matches = (holder[None, None, :] == route_ids[:, :, None]).astype(jnp.int32)
    target = jnp.sum(matches * slot_ids[None, None, :], axis=2)
    onehot = matches.reshape(tokens_here * top_count, groups)
    running = jnp.cumsum(onehot, axis=0) - 1
    position = jnp.sum(onehot * running, axis=1).reshape(tokens_here, top_count)
    row_index = target * capacity + position
    buffer_rows = jnp.arange(groups * capacity, dtype=jnp.int32)
    row_hits = buffer_rows[:, None, None] == row_index[None, :, :]
    dispatch = jnp.sum(row_hits.astype(jnp.float32), axis=2).astype(jnp.bfloat16)
    token_hits = row_index[:, :, None] == buffer_rows[None, None, :]
    combine = jnp.sum(
        jnp.where(token_hits, route_weight[:, :, None], jnp.zeros((), jnp.bfloat16)), axis=1
    )
    return (dispatch, combine, capacity)


def contract_last(left, right):
    return lax.dot_general(
        left, right, (((1,), (1,)), ((), ())), preferred_element_type=jnp.float32
    )


def pack_weights(gate, up, down, groups):
    rows, width = gate.shape
    depth, narrow_width = down.shape
    gate_c = gate.reshape(rows, width // LANES, LANES).transpose(1, 0, 2)
    up_c = up.reshape(rows, width // LANES, LANES).transpose(1, 0, 2)
    down_c = (
        down.reshape(depth // rows, rows, narrow_width // LANES, LANES)
        .transpose(0, 2, 1, 3)
        .reshape(-1, rows, LANES)
    )
    stacked = jnp.concatenate([gate_c, up_c, down_c], axis=0)
    return stacked.reshape(groups, -1, LANES)


def unpack_weights(packed, gate_shape, down_shape):
    rows, width = gate_shape
    depth, narrow_width = down_shape
    chunks = packed.reshape(-1, rows, LANES)
    n_gate = width // LANES
    gate = chunks[:n_gate].transpose(1, 0, 2).reshape(rows, width)
    up = chunks[n_gate : 2 * n_gate].transpose(1, 0, 2).reshape(rows, width)
    down = (
        chunks[2 * n_gate :]
        .reshape(depth // rows, narrow_width // LANES, rows, LANES)
        .transpose(0, 2, 1, 3)
        .reshape(depth, narrow_width)
    )
    return gate, up, down


def spread_weights(gate, up, down, groups):
    packed = pack_weights(gate, up, down, groups)
    return lax.all_to_all(packed, "expert", split_axis=0, concat_axis=0, tiled=True)


def finish_exchange(spread, partner, gate_shape, down_shape):
    ordered = jnp.take(spread, partner, axis=0, mode="clip")
    arrived = lax.all_to_all(ordered, "expert", split_axis=0, concat_axis=0, tiled=True)
    return unpack_weights(arrived, gate_shape, down_shape)


def body(tokens, route_ids, route_weight, partner, old_place, gate_weight, up_weight, down_weight):
    groups = lax.axis_size("expert")
    half = lax.axis_index("zlo")
    gate_block = gate_weight[0]
    up_block = up_weight[0]
    down_block = down_weight[0]

    spread = spread_weights(gate_block, up_block, down_block, groups)

    rows, width = gate_block.shape
    pair = [(0, 1), (1, 0)]
    gate_halves = gate_block.reshape(rows, 2, width // 2)
    up_halves = up_block.reshape(rows, 2, width // 2)
    keep = jnp.concatenate(
        [
            lax.dynamic_index_in_dim(gate_halves, half, axis=1, keepdims=False),
            lax.dynamic_index_in_dim(up_halves, half, axis=1, keepdims=False),
        ],
        axis=0,
    )
    give = jnp.concatenate(
        [
            lax.dynamic_index_in_dim(gate_halves, 1 - half, axis=1, keepdims=False),
            lax.dynamic_index_in_dim(up_halves, 1 - half, axis=1, keepdims=False),
        ],
        axis=0,
    )
    taken = lax.ppermute(give, "zlo", pair)

    dispatch, combine, capacity = slot_layout(route_ids, route_weight, old_place, groups)
    outgoing = jnp.dot(dispatch, tokens, preferred_element_type=jnp.float32).astype(jnp.bfloat16)
    arrived_rows = lax.all_to_all(
        outgoing.reshape(groups, capacity, -1), "expert", split_axis=0, concat_axis=0, tiled=True
    )
    taken, arrived_rows = lax.optimization_barrier((taken, arrived_rows))
    slice_rows = arrived_rows.reshape(-1, arrived_rows.shape[2])
    half_rows = lax.all_gather(slice_rows, "x", axis=1, tiled=True)
    own_part = contract_last(half_rows, keep)
    other_part = contract_last(half_rows, taken)
    spread, own_part, other_part = lax.optimization_barrier((spread, own_part, other_part))
    new_gate, new_up, new_down = finish_exchange(spread, partner, gate_block.shape, down_block.shape)
    back = lax.ppermute(other_part, "zlo", pair)
    sums = own_part + back
    gate_sum = sums[:, :rows]
    up_sum = sums[:, rows:]
    hidden = (jax.nn.silu(gate_sum) * up_sum).astype(jnp.bfloat16)
    produced = (
        jnp.dot(
            lax.all_gather(hidden, ("zlo", "x"), axis=1, tiled=True),
            down_block,
            preferred_element_type=jnp.float32,
        )
        .astype(jnp.bfloat16)
        .reshape(groups, capacity, -1)
    )
    returned = lax.all_to_all(produced, "expert", split_axis=0, concat_axis=0, tiled=True)
    layer_out = jnp.dot(
        combine, returned.reshape(-1, returned.shape[2]), preferred_element_type=jnp.float32
    ).astype(jnp.bfloat16)
    return (
        layer_out,
        new_gate.reshape(gate_weight.shape),
        new_up.reshape(up_weight.shape),
        new_down.reshape(down_weight.shape),
    )


def solution(mesh):
    expert_size, narrow_size = mesh.devices.shape
    split_mesh = Mesh(
        mesh.devices.reshape(expert_size, 2, narrow_size // 2), ("expert", "zlo", "x")
    )
    narrow = ("zlo", "x")
    return jax.shard_map(
        body,
        mesh=split_mesh,
        in_specs=(
            P("expert", narrow),
            P("expert", None),
            P("expert", None),
            P(),
            P(),
            P("expert", narrow, None),
            P("expert", narrow, None),
            P("expert", None, narrow),
        ),
        out_specs=(
            P("expert", narrow),
            P("expert", narrow, None),
            P("expert", narrow, None),
            P("expert", None, narrow),
        ),
        check_vma=False,
    )
```

```python
import jax
import jax.numpy as jnp
from jax import lax
from jax.sharding import Mesh, PartitionSpec as P

LANES = 128


def slot_layout(route_ids, route_weight, holder, groups):
    tokens_here, top_count = route_ids.shape
    capacity = 2 * tokens_here * top_count // groups
    slot_ids = jnp.arange(groups, dtype=jnp.int32)
    matches = (holder[None, None, :] == route_ids[:, :, None]).astype(jnp.int32)
    target = jnp.sum(matches * slot_ids[None, None, :], axis=2)
    onehot = matches.reshape(tokens_here * top_count, groups)
    running = jnp.cumsum(onehot, axis=0) - 1
    position = jnp.sum(onehot * running, axis=1).reshape(tokens_here, top_count)
    row_index = target * capacity + position
    buffer_rows = jnp.arange(groups * capacity, dtype=jnp.int32)
    row_hits = buffer_rows[:, None, None] == row_index[None, :, :]
    dispatch = jnp.sum(row_hits.astype(jnp.float32), axis=2).astype(jnp.bfloat16)
    token_hits = row_index[:, :, None] == buffer_rows[None, None, :]
    combine = jnp.sum(
        jnp.where(token_hits, route_weight[:, :, None], jnp.zeros((), jnp.bfloat16)), axis=1
    )
    return (dispatch, combine, capacity)


def contract_last(left, right):
    return lax.dot_general(
        left, right, (((1,), (1,)), ((), ())), preferred_element_type=jnp.float32
    )


def pack_weights(gate, up, down, groups):
    rows, width = gate.shape
    depth, narrow_width = down.shape
    gate_c = gate.reshape(rows, width // LANES, LANES).transpose(1, 0, 2)
    up_c = up.reshape(rows, width // LANES, LANES).transpose(1, 0, 2)
    down_c = (
        down.reshape(depth // rows, rows, narrow_width // LANES, LANES)
        .transpose(0, 2, 1, 3)
        .reshape(-1, rows, LANES)
    )
    stacked = jnp.concatenate([gate_c, up_c, down_c], axis=0)
    return stacked.reshape(groups, -1, LANES)


def unpack_weights(packed, gate_shape, down_shape):
    rows, width = gate_shape
    depth, narrow_width = down_shape
    chunks = packed.reshape(-1, rows, LANES)
    n_gate = width // LANES
    gate = chunks[:n_gate].transpose(1, 0, 2).reshape(rows, width)
    up = chunks[n_gate : 2 * n_gate].transpose(1, 0, 2).reshape(rows, width)
    down = (
        chunks[2 * n_gate :]
        .reshape(depth // rows, narrow_width // LANES, rows, LANES)
        .transpose(0, 2, 1, 3)
        .reshape(depth, narrow_width)
    )
    return gate, up, down


def to_lanes(block, groups):
    return block.reshape(groups, -1, LANES)


def body(tokens, route_ids, route_weight, partner, old_place, gate_weight, up_weight, down_weight):
    groups = lax.axis_size("expert")
    half = lax.axis_index("zlo")
    gate_block = gate_weight[0]
    up_block = up_weight[0]
    down_block = down_weight[0]
    rows, width = gate_block.shape
    depth, narrow_width = down_block.shape
    pair = [(0, 1), (1, 0)]

    gate_halves = gate_block.reshape(rows, 2, width // 2)
    up_halves = up_block.reshape(rows, 2, width // 2)
    keep = jnp.concatenate(
        [
            lax.dynamic_index_in_dim(gate_halves, half, axis=1, keepdims=False),
            lax.dynamic_index_in_dim(up_halves, half, axis=1, keepdims=False),
        ],
        axis=0,
    )
    give = jnp.concatenate(
        [
            lax.dynamic_index_in_dim(gate_halves, 1 - half, axis=1, keepdims=False),
            lax.dynamic_index_in_dim(up_halves, 1 - half, axis=1, keepdims=False),
        ],
        axis=0,
    )
    taken = lax.ppermute(give, "zlo", pair)

    dispatch, combine, capacity = slot_layout(route_ids, route_weight, old_place, groups)
    outgoing = jnp.dot(dispatch, tokens, preferred_element_type=jnp.float32).astype(jnp.bfloat16)
    packed = pack_weights(gate_block, up_block, down_block, groups)
    token_lanes = to_lanes(outgoing, groups)
    split_at = token_lanes.shape[1]
    first = lax.all_to_all(
        jnp.concatenate([token_lanes, packed], axis=1),
        "expert",
        split_axis=0,
        concat_axis=0,
        tiled=True,
    )
    slice_rows = first[:, :split_at].reshape(groups * capacity, narrow_width)
    spread = first[:, split_at:]

    pieces = lax.all_gather(slice_rows, "x", axis=0, tiled=False)
    keep3 = keep.reshape(keep.shape[0], pieces.shape[0], narrow_width)
    taken3 = taken.reshape(taken.shape[0], pieces.shape[0], narrow_width)
    own_part = lax.dot_general(
        pieces, keep3, (((0, 2), (1, 2)), ((), ())), preferred_element_type=jnp.float32
    )
    other_part = lax.dot_general(
        pieces, taken3, (((0, 2), (1, 2)), ((), ())), preferred_element_type=jnp.float32
    )
    back = lax.ppermute(other_part, "zlo", pair)
    sums = own_part + back
    gate_sum = sums[:, :rows]
    up_sum = sums[:, rows:]
    hidden = (jax.nn.silu(gate_sum) * up_sum).astype(jnp.bfloat16)
    hidden_all = lax.all_gather(hidden, ("zlo", "x"), axis=0, tiled=False)
    down3 = down_block.reshape(hidden_all.shape[0], rows, narrow_width)
    produced = lax.dot_general(
        hidden_all, down3, (((0, 2), (0, 1)), ((), ())), preferred_element_type=jnp.float32
    ).astype(jnp.bfloat16)

    ordered = jnp.take(spread, partner, axis=0, mode="clip")
    second = lax.all_to_all(
        jnp.concatenate([to_lanes(produced, groups), ordered], axis=1),
        "expert",
        split_axis=0,
        concat_axis=0,
        tiled=True,
    )
    returned = second[:, :split_at].reshape(groups * capacity, narrow_width)
    new_gate, new_up, new_down = unpack_weights(second[:, split_at:], gate_block.shape, down_block.shape)
    layer_out = jnp.dot(combine, returned, preferred_element_type=jnp.float32).astype(jnp.bfloat16)
    return (
        layer_out,
        new_gate.reshape(gate_weight.shape),
        new_up.reshape(up_weight.shape),
        new_down.reshape(down_weight.shape),
    )


def solution(mesh):
    expert_size, narrow_size = mesh.devices.shape
    split_mesh = Mesh(
        mesh.devices.reshape(expert_size, 2, narrow_size // 2), ("expert", "zlo", "x")
    )
    narrow = ("zlo", "x")
    return jax.shard_map(
        body,
        mesh=split_mesh,
        in_specs=(
            P("expert", narrow),
            P("expert", None),
            P("expert", None),
            P(),
            P(),
            P("expert", narrow, None),
            P("expert", narrow, None),
            P("expert", None, narrow),
        ),
        out_specs=(
            P("expert", narrow),
            P("expert", narrow, None),
            P("expert", narrow, None),
            P("expert", None, narrow),
        ),
        check_vma=False,
    )
```

```python
import jax
import jax.numpy as jnp
from jax import lax
from jax.sharding import Mesh, PartitionSpec as P

LANES = 128


def slot_layout(route_ids, route_weight, holder, groups):
    tokens_here, top_count = route_ids.shape
    capacity = 2 * tokens_here * top_count // groups
    slot_ids = jnp.arange(groups, dtype=jnp.int32)
    matches = (holder[None, None, :] == route_ids[:, :, None]).astype(jnp.int32)
    target = jnp.sum(matches * slot_ids[None, None, :], axis=2)
    onehot = matches.reshape(tokens_here * top_count, groups)
    running = jnp.cumsum(onehot, axis=0) - 1
    position = jnp.sum(onehot * running, axis=1).reshape(tokens_here, top_count)
    row_index = target * capacity + position
    buffer_rows = jnp.arange(groups * capacity, dtype=jnp.int32)
    row_hits = buffer_rows[:, None, None] == row_index[None, :, :]
    dispatch = jnp.sum(row_hits.astype(jnp.float32), axis=2).astype(jnp.bfloat16)
    token_hits = row_index[:, :, None] == buffer_rows[None, None, :]
    combine = jnp.sum(
        jnp.where(token_hits, route_weight[:, :, None], jnp.zeros((), jnp.bfloat16)), axis=1
    )
    return (dispatch, combine, capacity)


def contract_last(left, right):
    return lax.dot_general(
        left, right, (((1,), (1,)), ((), ())), preferred_element_type=jnp.float32
    )


def pack_weights(gate, up, down, groups):
    rows, width = gate.shape
    depth, narrow_width = down.shape
    gate_c = gate.reshape(rows, width // LANES, LANES).transpose(1, 0, 2)
    up_c = up.reshape(rows, width // LANES, LANES).transpose(1, 0, 2)
    down_c = (
        down.reshape(depth // rows, rows, narrow_width // LANES, LANES)
        .transpose(0, 2, 1, 3)
        .reshape(-1, rows, LANES)
    )
    stacked = jnp.concatenate([gate_c, up_c, down_c], axis=0)
    return stacked.reshape(groups, -1, LANES)


def unpack_weights(packed, gate_shape, down_shape):
    rows, width = gate_shape
    depth, narrow_width = down_shape
    chunks = packed.reshape(-1, rows, LANES)
    n_gate = width // LANES
    gate = chunks[:n_gate].transpose(1, 0, 2).reshape(rows, width)
    up = chunks[n_gate : 2 * n_gate].transpose(1, 0, 2).reshape(rows, width)
    down = (
        chunks[2 * n_gate :]
        .reshape(depth // rows, narrow_width // LANES, rows, LANES)
        .transpose(0, 2, 1, 3)
        .reshape(depth, narrow_width)
    )
    return gate, up, down


def to_lanes(block, groups):
    return block.reshape(groups, -1, LANES)


def ring_gather(value, axis, size, index):
    pieces = [value]
    for shift in range(1, size):
        pieces.append(lax.ppermute(value, axis, [(i, (i + shift) % size) for i in range(size)]))
    sources = (index - jnp.arange(size, dtype=jnp.int32)) % size
    return jnp.stack(pieces, axis=0), sources


def body(tokens, route_ids, route_weight, partner, old_place, gate_weight, up_weight, down_weight):
    groups = lax.axis_size("expert")
    half = lax.axis_index("zlo")
    column = lax.axis_index("x")
    columns = lax.axis_size("x")
    narrow_count = lax.axis_size("zlo") * columns
    narrow_index = half * columns + column
    gate_block = gate_weight[0]
    up_block = up_weight[0]
    down_block = down_weight[0]
    rows, width = gate_block.shape
    depth, narrow_width = down_block.shape
    pair = [(0, 1), (1, 0)]

    gate_halves = gate_block.reshape(rows, 2, width // 2)
    up_halves = up_block.reshape(rows, 2, width // 2)
    keep = jnp.concatenate(
        [
            lax.dynamic_index_in_dim(gate_halves, half, axis=1, keepdims=False),
            lax.dynamic_index_in_dim(up_halves, half, axis=1, keepdims=False),
        ],
        axis=0,
    )
    give = jnp.concatenate(
        [
            lax.dynamic_index_in_dim(gate_halves, 1 - half, axis=1, keepdims=False),
            lax.dynamic_index_in_dim(up_halves, 1 - half, axis=1, keepdims=False),
        ],
        axis=0,
    )
    both = lax.all_gather(give, "zlo", axis=0, tiled=False)
    taken = lax.dynamic_index_in_dim(both, 1 - half, axis=0, keepdims=False)

    dispatch, combine, capacity = slot_layout(route_ids, route_weight, old_place, groups)
    outgoing = jnp.dot(dispatch, tokens, preferred_element_type=jnp.float32).astype(jnp.bfloat16)
    packed = pack_weights(gate_block, up_block, down_block, groups)
    token_lanes = to_lanes(outgoing, groups)
    split_at = token_lanes.shape[1]
    first = lax.all_to_all(
        jnp.concatenate([token_lanes, packed], axis=1),
        "expert",
        split_axis=0,
        concat_axis=0,
        tiled=True,
    )
    slice_rows = first[:, :split_at].reshape(groups * capacity, narrow_width)
    spread = first[:, split_at:]
    ordered = jnp.take(spread, partner, axis=0, mode="clip")
    arrived = lax.all_to_all(ordered, "expert", split_axis=0, concat_axis=0, tiled=True)

    pieces, sources = ring_gather(slice_rows, "x", columns, column)
    keep3 = jnp.take(keep.reshape(keep.shape[0], columns, narrow_width), sources, axis=1, mode="clip")
    taken3 = jnp.take(
        taken.reshape(taken.shape[0], columns, narrow_width), sources, axis=1, mode="clip"
    )
    own_part = lax.dot_general(
        pieces, keep3, (((0, 2), (1, 2)), ((), ())), preferred_element_type=jnp.float32
    )
    other_part = lax.dot_general(
        pieces, taken3, (((0, 2), (1, 2)), ((), ())), preferred_element_type=jnp.float32
    )
    back = lax.ppermute(other_part, "zlo", pair)
    sums = own_part + back
    gate_sum = sums[:, :rows]
    up_sum = sums[:, rows:]
    hidden = (jax.nn.silu(gate_sum) * up_sum).astype(jnp.bfloat16)
    hidden_all, owners = ring_gather(hidden, ("zlo", "x"), narrow_count, narrow_index)
    down3 = jnp.take(down_block.reshape(narrow_count, rows, narrow_width), owners, axis=0, mode="clip")
    produced = lax.dot_general(
        hidden_all, down3, (((0, 2), (0, 1)), ((), ())), preferred_element_type=jnp.float32
    ).astype(jnp.bfloat16)

    produced, arrived = lax.optimization_barrier((produced, arrived))
    returned = lax.all_to_all(
        produced.reshape(groups, capacity, -1), "expert", split_axis=0, concat_axis=0, tiled=True
    ).reshape(groups * capacity, narrow_width)
    new_gate, new_up, new_down = unpack_weights(arrived, gate_block.shape, down_block.shape)
    layer_out = jnp.dot(combine, returned, preferred_element_type=jnp.float32).astype(jnp.bfloat16)
    return (
        layer_out,
        new_gate.reshape(gate_weight.shape),
        new_up.reshape(up_weight.shape),
        new_down.reshape(down_weight.shape),
    )


def solution(mesh):
    expert_size, narrow_size = mesh.devices.shape
    split_mesh = Mesh(
        mesh.devices.reshape(expert_size, 2, narrow_size // 2), ("expert", "zlo", "x")
    )
    narrow = ("zlo", "x")
    return jax.shard_map(
        body,
        mesh=split_mesh,
        in_specs=(
            P("expert", narrow),
            P("expert", None),
            P("expert", None),
            P(),
            P(),
            P("expert", narrow, None),
            P("expert", narrow, None),
            P("expert", None, narrow),
        ),
        out_specs=(
            P("expert", narrow),
            P("expert", narrow, None),
            P("expert", narrow, None),
            P("expert", None, narrow),
        ),
        check_vma=False,
    )
```

```python
import jax
import jax.numpy as jnp
from jax import lax
from jax.sharding import Mesh, PartitionSpec as P

LANES = 128


def slot_layout(route_ids, route_weight, holder, groups):
    tokens_here, top_count = route_ids.shape
    capacity = 2 * tokens_here * top_count // groups
    slot_ids = jnp.arange(groups, dtype=jnp.int32)
    matches = (holder[None, None, :] == route_ids[:, :, None]).astype(jnp.int32)
    target = jnp.sum(matches * slot_ids[None, None, :], axis=2)
    onehot = matches.reshape(tokens_here * top_count, groups)
    running = jnp.cumsum(onehot, axis=0) - 1
    position = jnp.sum(onehot * running, axis=1).reshape(tokens_here, top_count)
    row_index = target * capacity + position
    buffer_rows = jnp.arange(groups * capacity, dtype=jnp.int32)
    row_hits = buffer_rows[:, None, None] == row_index[None, :, :]
    dispatch = jnp.sum(row_hits.astype(jnp.float32), axis=2).astype(jnp.bfloat16)
    token_hits = row_index[:, :, None] == buffer_rows[None, None, :]
    combine = jnp.sum(
        jnp.where(token_hits, route_weight[:, :, None], jnp.zeros((), jnp.bfloat16)), axis=1
    )
    return (dispatch, combine, capacity)


def contract_last(left, right):
    return lax.dot_general(
        left, right, (((1,), (1,)), ((), ())), preferred_element_type=jnp.float32
    )


def pack_weights(gate, up, down, groups):
    rows, width = gate.shape
    depth, narrow_width = down.shape
    gate_c = gate.reshape(rows, width // LANES, LANES).transpose(1, 0, 2)
    up_c = up.reshape(rows, width // LANES, LANES).transpose(1, 0, 2)
    down_c = (
        down.reshape(depth // rows, rows, narrow_width // LANES, LANES)
        .transpose(0, 2, 1, 3)
        .reshape(-1, rows, LANES)
    )
    stacked = jnp.concatenate([gate_c, up_c, down_c], axis=0)
    return stacked.reshape(groups, -1, LANES)


def unpack_weights(packed, gate_shape, down_shape):
    rows, width = gate_shape
    depth, narrow_width = down_shape
    chunks = packed.reshape(-1, rows, LANES)
    n_gate = width // LANES
    gate = chunks[:n_gate].transpose(1, 0, 2).reshape(rows, width)
    up = chunks[n_gate : 2 * n_gate].transpose(1, 0, 2).reshape(rows, width)
    down = (
        chunks[2 * n_gate :]
        .reshape(depth // rows, narrow_width // LANES, rows, LANES)
        .transpose(0, 2, 1, 3)
        .reshape(depth, narrow_width)
    )
    return gate, up, down


def to_lanes(block, groups):
    return block.reshape(groups, -1, LANES)


def ring_gather(value, axis, size, index):
    pieces = [value]
    for shift in range(1, size):
        pieces.append(lax.ppermute(value, axis, [(i, (i + shift) % size) for i in range(size)]))
    sources = (index - jnp.arange(size, dtype=jnp.int32)) % size
    return jnp.stack(pieces, axis=0), sources


def body(tokens, route_ids, route_weight, partner, old_place, gate_weight, up_weight, down_weight):
    groups = lax.axis_size("expert")
    half = lax.axis_index("zlo")
    column = lax.axis_index("x")
    columns = lax.axis_size("x")
    narrow_count = lax.axis_size("zlo") * columns
    narrow_index = half * columns + column
    gate_block = gate_weight[0]
    up_block = up_weight[0]
    down_block = down_weight[0]
    rows, width = gate_block.shape
    depth, narrow_width = down_block.shape
    pair = [(0, 1), (1, 0)]

    gate_halves = gate_block.reshape(rows, 2, width // 2)
    up_halves = up_block.reshape(rows, 2, width // 2)
    keep = jnp.concatenate(
        [
            lax.dynamic_index_in_dim(gate_halves, half, axis=1, keepdims=False),
            lax.dynamic_index_in_dim(up_halves, half, axis=1, keepdims=False),
        ],
        axis=0,
    )
    give = jnp.concatenate(
        [
            lax.dynamic_index_in_dim(gate_halves, 1 - half, axis=1, keepdims=False),
            lax.dynamic_index_in_dim(up_halves, 1 - half, axis=1, keepdims=False),
        ],
        axis=0,
    )
    both = lax.all_gather(give, "zlo", axis=0, tiled=False)
    taken = lax.dynamic_index_in_dim(both, 1 - half, axis=0, keepdims=False)

    dispatch, combine, capacity = slot_layout(route_ids, route_weight, old_place, groups)
    outgoing = jnp.dot(dispatch, tokens, preferred_element_type=jnp.float32).astype(jnp.bfloat16)
    packed = pack_weights(gate_block, up_block, down_block, groups)
    token_lanes = to_lanes(outgoing, groups)
    split_at = token_lanes.shape[1]
    first = lax.all_to_all(
        jnp.concatenate([token_lanes, packed], axis=1),
        "expert",
        split_axis=0,
        concat_axis=0,
        tiled=True,
    )
    slice_rows = first[:, :split_at].reshape(groups * capacity, narrow_width)
    spread = first[:, split_at:]

    pieces, sources = ring_gather(slice_rows, "x", columns, column)
    keep3 = jnp.take(keep.reshape(keep.shape[0], columns, narrow_width), sources, axis=1, mode="clip")
    taken3 = jnp.take(
        taken.reshape(taken.shape[0], columns, narrow_width), sources, axis=1, mode="clip"
    )
    own_part = lax.dot_general(
        pieces, keep3, (((0, 2), (1, 2)), ((), ())), preferred_element_type=jnp.float32
    )
    other_part = lax.dot_general(
        pieces, taken3, (((0, 2), (1, 2)), ((), ())), preferred_element_type=jnp.float32
    )
    back = lax.ppermute(other_part, "zlo", pair)
    sums = own_part + back
    gate_sum = sums[:, :rows]
    up_sum = sums[:, rows:]
    hidden = (jax.nn.silu(gate_sum) * up_sum).astype(jnp.bfloat16)
    hidden_all, owners = ring_gather(hidden, ("zlo", "x"), narrow_count, narrow_index)
    down3 = jnp.take(down_block.reshape(narrow_count, rows, narrow_width), owners, axis=0, mode="clip")
    produced = lax.dot_general(
        hidden_all, down3, (((0, 2), (0, 1)), ((), ())), preferred_element_type=jnp.float32
    ).astype(jnp.bfloat16)

    ordered = jnp.take(spread, partner, axis=0, mode="clip")
    second = lax.all_to_all(
        jnp.concatenate([to_lanes(produced, groups), ordered], axis=1),
        "expert",
        split_axis=0,
        concat_axis=0,
        tiled=True,
    )
    returned = second[:, :split_at].reshape(groups * capacity, narrow_width)
    new_gate, new_up, new_down = unpack_weights(second[:, split_at:], gate_block.shape, down_block.shape)
    layer_out = jnp.dot(combine, returned, preferred_element_type=jnp.float32).astype(jnp.bfloat16)
    return (
        layer_out,
        new_gate.reshape(gate_weight.shape),
        new_up.reshape(up_weight.shape),
        new_down.reshape(down_weight.shape),
    )


def solution(mesh):
    expert_size, narrow_size = mesh.devices.shape
    split_mesh = Mesh(
        mesh.devices.reshape(expert_size, 2, narrow_size // 2), ("expert", "zlo", "x")
    )
    narrow = ("zlo", "x")
    return jax.shard_map(
        body,
        mesh=split_mesh,
        in_specs=(
            P("expert", narrow),
            P("expert", None),
            P("expert", None),
            P(),
            P(),
            P("expert", narrow, None),
            P("expert", narrow, None),
            P("expert", None, narrow),
        ),
        out_specs=(
            P("expert", narrow),
            P("expert", narrow, None),
            P("expert", narrow, None),
            P("expert", None, narrow),
        ),
        check_vma=False,
    )
```

```python
import jax
import jax.numpy as jnp
from jax import lax
from jax.sharding import Mesh, PartitionSpec as P

LANES = 128


def slot_layout(route_ids, route_weight, holder, groups):
    tokens_here, top_count = route_ids.shape
    capacity = 2 * tokens_here * top_count // groups
    slot_ids = jnp.arange(groups, dtype=jnp.int32)
    matches = (holder[None, None, :] == route_ids[:, :, None]).astype(jnp.int32)
    target = jnp.sum(matches * slot_ids[None, None, :], axis=2)
    onehot = matches.reshape(tokens_here * top_count, groups)
    running = jnp.cumsum(onehot, axis=0) - 1
    position = jnp.sum(onehot * running, axis=1).reshape(tokens_here, top_count)
    row_index = target * capacity + position
    buffer_rows = jnp.arange(groups * capacity, dtype=jnp.int32)
    row_hits = buffer_rows[:, None, None] == row_index[None, :, :]
    dispatch = jnp.sum(row_hits.astype(jnp.float32), axis=2).astype(jnp.bfloat16)
    token_hits = row_index[:, :, None] == buffer_rows[None, None, :]
    combine = jnp.sum(
        jnp.where(token_hits, route_weight[:, :, None], jnp.zeros((), jnp.bfloat16)), axis=1
    )
    return (dispatch, combine, capacity)


def contract_last(left, right):
    return lax.dot_general(
        left, right, (((1,), (1,)), ((), ())), preferred_element_type=jnp.float32
    )


def pack_weights(gate, up, down, groups):
    rows, width = gate.shape
    depth, narrow_width = down.shape
    gate_c = gate.reshape(rows, width // LANES, LANES).transpose(1, 0, 2)
    up_c = up.reshape(rows, width // LANES, LANES).transpose(1, 0, 2)
    down_c = (
        down.reshape(depth // rows, rows, narrow_width // LANES, LANES)
        .transpose(0, 2, 1, 3)
        .reshape(-1, rows, LANES)
    )
    stacked = jnp.concatenate([gate_c, up_c, down_c], axis=0)
    return stacked.reshape(groups, -1, LANES)


def unpack_weights(packed, gate_shape, down_shape):
    rows, width = gate_shape
    depth, narrow_width = down_shape
    chunks = packed.reshape(-1, rows, LANES)
    n_gate = width // LANES
    gate = chunks[:n_gate].transpose(1, 0, 2).reshape(rows, width)
    up = chunks[n_gate : 2 * n_gate].transpose(1, 0, 2).reshape(rows, width)
    down = (
        chunks[2 * n_gate :]
        .reshape(depth // rows, narrow_width // LANES, rows, LANES)
        .transpose(0, 2, 1, 3)
        .reshape(depth, narrow_width)
    )
    return gate, up, down


def to_lanes(block, groups):
    return block.reshape(groups, -1, LANES)


def ring_gather(value, axis, size, index):
    pieces = [value]
    for shift in range(1, size):
        pieces.append(lax.ppermute(value, axis, [(i, (i + shift) % size) for i in range(size)]))
    sources = (index - jnp.arange(size, dtype=jnp.int32)) % size
    return jnp.stack(pieces, axis=0), sources


def body(tokens, route_ids, route_weight, partner, old_place, gate_weight, up_weight, down_weight):
    groups = lax.axis_size("expert")
    half = lax.axis_index("zlo")
    column = lax.axis_index("x")
    columns = lax.axis_size("x")
    narrow_count = lax.axis_size("zlo") * columns
    narrow_index = half * columns + column
    gate_block = gate_weight[0]
    up_block = up_weight[0]
    down_block = down_weight[0]
    rows, width = gate_block.shape
    depth, narrow_width = down_block.shape
    pair = [(0, 1), (1, 0)]

    gate_halves = gate_block.reshape(rows, 2, width // 2)
    up_halves = up_block.reshape(rows, 2, width // 2)
    keep = jnp.concatenate(
        [
            lax.dynamic_index_in_dim(gate_halves, half, axis=1, keepdims=False),
            lax.dynamic_index_in_dim(up_halves, half, axis=1, keepdims=False),
        ],
        axis=0,
    )
    give = jnp.concatenate(
        [
            lax.dynamic_index_in_dim(gate_halves, 1 - half, axis=1, keepdims=False),
            lax.dynamic_index_in_dim(up_halves, 1 - half, axis=1, keepdims=False),
        ],
        axis=0,
    )
    taken = lax.ppermute(give, "zlo", pair)

    dispatch, combine, capacity = slot_layout(route_ids, route_weight, old_place, groups)
    outgoing = jnp.dot(dispatch, tokens, preferred_element_type=jnp.float32).astype(jnp.bfloat16)
    packed = pack_weights(gate_block, up_block, down_block, groups)
    token_lanes = to_lanes(outgoing, groups)
    split_at = token_lanes.shape[1]
    first = lax.all_to_all(
        jnp.concatenate([token_lanes, packed], axis=1),
        "expert",
        split_axis=0,
        concat_axis=0,
        tiled=True,
    )
    slice_rows = first[:, :split_at].reshape(groups * capacity, narrow_width)
    spread = first[:, split_at:]
    ordered = jnp.take(spread, partner, axis=0, mode="clip")
    arrived = lax.all_to_all(ordered, "expert", split_axis=0, concat_axis=0, tiled=True)

    pieces, sources = ring_gather(slice_rows, "x", columns, column)
    keep3 = jnp.take(keep.reshape(keep.shape[0], columns, narrow_width), sources, axis=1, mode="clip")
    taken3 = jnp.take(
        taken.reshape(taken.shape[0], columns, narrow_width), sources, axis=1, mode="clip"
    )
    own_part = lax.dot_general(
        pieces, keep3, (((0, 2), (1, 2)), ((), ())), preferred_element_type=jnp.float32
    )
    other_part = lax.dot_general(
        pieces, taken3, (((0, 2), (1, 2)), ((), ())), preferred_element_type=jnp.float32
    )
    back = lax.ppermute(other_part, "zlo", pair)
    sums = own_part + back
    gate_sum = sums[:, :rows]
    up_sum = sums[:, rows:]
    hidden = (jax.nn.silu(gate_sum) * up_sum).astype(jnp.bfloat16)
    hidden_all, owners = ring_gather(hidden, ("zlo", "x"), narrow_count, narrow_index)
    down3 = jnp.take(down_block.reshape(narrow_count, rows, narrow_width), owners, axis=0, mode="clip")
    produced = lax.dot_general(
        hidden_all, down3, (((0, 2), (0, 1)), ((), ())), preferred_element_type=jnp.float32
    ).astype(jnp.bfloat16)

    produced, arrived = lax.optimization_barrier((produced, arrived))
    returned = lax.all_to_all(
        produced.reshape(groups, capacity, -1), "expert", split_axis=0, concat_axis=0, tiled=True
    ).reshape(groups * capacity, narrow_width)
    new_gate, new_up, new_down = unpack_weights(arrived, gate_block.shape, down_block.shape)
    layer_out = jnp.dot(combine, returned, preferred_element_type=jnp.float32).astype(jnp.bfloat16)
    return (
        layer_out,
        new_gate.reshape(gate_weight.shape),
        new_up.reshape(up_weight.shape),
        new_down.reshape(down_weight.shape),
    )


def solution(mesh):
    expert_size, narrow_size = mesh.devices.shape
    split_mesh = Mesh(
        mesh.devices.reshape(expert_size, 2, narrow_size // 2), ("expert", "zlo", "x")
    )
    narrow = ("zlo", "x")
    return jax.shard_map(
        body,
        mesh=split_mesh,
        in_specs=(
            P("expert", narrow),
            P("expert", None),
            P("expert", None),
            P(),
            P(),
            P("expert", narrow, None),
            P("expert", narrow, None),
            P("expert", None, narrow),
        ),
        out_specs=(
            P("expert", narrow),
            P("expert", narrow, None),
            P("expert", narrow, None),
            P("expert", None, narrow),
        ),
        check_vma=False,
    )
```

```python
import jax
import jax.numpy as jnp
from jax import lax
from jax.sharding import Mesh, PartitionSpec as P

LANES = 128


def slot_layout(route_ids, route_weight, holder, groups):
    tokens_here, top_count = route_ids.shape
    capacity = 2 * tokens_here * top_count // groups
    slot_ids = jnp.arange(groups, dtype=jnp.int32)
    matches = (holder[None, None, :] == route_ids[:, :, None]).astype(jnp.int32)
    target = jnp.sum(matches * slot_ids[None, None, :], axis=2)
    onehot = matches.reshape(tokens_here * top_count, groups)
    running = jnp.cumsum(onehot, axis=0) - 1
    position = jnp.sum(onehot * running, axis=1).reshape(tokens_here, top_count)
    row_index = target * capacity + position
    buffer_rows = jnp.arange(groups * capacity, dtype=jnp.int32)
    row_hits = buffer_rows[:, None, None] == row_index[None, :, :]
    dispatch = jnp.sum(row_hits.astype(jnp.float32), axis=2).astype(jnp.bfloat16)
    token_hits = row_index[:, :, None] == buffer_rows[None, None, :]
    combine = jnp.sum(
        jnp.where(token_hits, route_weight[:, :, None], jnp.zeros((), jnp.bfloat16)), axis=1
    )
    return (dispatch, combine, capacity)


def contract_last(left, right):
    return lax.dot_general(
        left, right, (((1,), (1,)), ((), ())), preferred_element_type=jnp.float32
    )


def pack_weights(gate, up, down, groups):
    rows, width = gate.shape
    depth, narrow_width = down.shape
    gate_c = gate.reshape(rows, width // LANES, LANES).transpose(1, 0, 2)
    up_c = up.reshape(rows, width // LANES, LANES).transpose(1, 0, 2)
    down_c = (
        down.reshape(depth // rows, rows, narrow_width // LANES, LANES)
        .transpose(0, 2, 1, 3)
        .reshape(-1, rows, LANES)
    )
    stacked = jnp.concatenate([gate_c, up_c, down_c], axis=0)
    return stacked.reshape(groups, -1, LANES)


def unpack_weights(packed, gate_shape, down_shape):
    rows, width = gate_shape
    depth, narrow_width = down_shape
    chunks = packed.reshape(-1, rows, LANES)
    n_gate = width // LANES
    gate = chunks[:n_gate].transpose(1, 0, 2).reshape(rows, width)
    up = chunks[n_gate : 2 * n_gate].transpose(1, 0, 2).reshape(rows, width)
    down = (
        chunks[2 * n_gate :]
        .reshape(depth // rows, narrow_width // LANES, rows, LANES)
        .transpose(0, 2, 1, 3)
        .reshape(depth, narrow_width)
    )
    return gate, up, down


def to_lanes(block, groups):
    return block.reshape(groups, -1, LANES)


def ring_gather(value, axis, size, index):
    pieces = [value]
    for shift in range(1, size):
        pieces.append(lax.ppermute(value, axis, [(i, (i + shift) % size) for i in range(size)]))
    sources = (index - jnp.arange(size, dtype=jnp.int32)) % size
    return jnp.stack(pieces, axis=0), sources


def body(tokens, route_ids, route_weight, partner, old_place, gate_weight, up_weight, down_weight):
    groups = lax.axis_size("expert")
    half = lax.axis_index("zlo")
    column = lax.axis_index("x")
    columns = lax.axis_size("x")
    narrow_count = lax.axis_size("zlo") * columns
    narrow_index = half * columns + column
    gate_block = gate_weight[0]
    up_block = up_weight[0]
    down_block = down_weight[0]
    rows, width = gate_block.shape
    depth, narrow_width = down_block.shape
    pair = [(0, 1), (1, 0)]

    gate_halves = gate_block.reshape(rows, 2, width // 2)
    up_halves = up_block.reshape(rows, 2, width // 2)
    keep = jnp.concatenate(
        [
            lax.dynamic_index_in_dim(gate_halves, half, axis=1, keepdims=False),
            lax.dynamic_index_in_dim(up_halves, half, axis=1, keepdims=False),
        ],
        axis=0,
    )
    give = jnp.concatenate(
        [
            lax.dynamic_index_in_dim(gate_halves, 1 - half, axis=1, keepdims=False),
            lax.dynamic_index_in_dim(up_halves, 1 - half, axis=1, keepdims=False),
        ],
        axis=0,
    )
    taken = lax.ppermute(give, "zlo", pair)

    dispatch, combine, capacity = slot_layout(route_ids, route_weight, old_place, groups)
    outgoing = jnp.dot(dispatch, tokens, preferred_element_type=jnp.float32).astype(jnp.bfloat16)
    packed = pack_weights(gate_block, up_block, down_block, groups)
    token_lanes = to_lanes(outgoing, groups)
    split_at = token_lanes.shape[1]
    first = lax.all_to_all(
        jnp.concatenate([token_lanes, packed], axis=1),
        "expert",
        split_axis=0,
        concat_axis=0,
        tiled=True,
    )
    slice_rows = first[:, :split_at].reshape(groups * capacity, narrow_width)
    spread = first[:, split_at:]
    ordered = jnp.take(spread, partner, axis=0, mode="clip")
    arrived = lax.all_to_all(ordered, "expert", split_axis=0, concat_axis=0, tiled=True)

    pieces, sources = ring_gather(slice_rows, "x", columns, column)
    keep3 = jnp.take(keep.reshape(keep.shape[0], columns, narrow_width), sources, axis=1, mode="clip")
    taken3 = jnp.take(
        taken.reshape(taken.shape[0], columns, narrow_width), sources, axis=1, mode="clip"
    )
    own_part = lax.dot_general(
        pieces, keep3, (((0, 2), (1, 2)), ((), ())), preferred_element_type=jnp.float32
    )
    other_part = lax.dot_general(
        pieces, taken3, (((0, 2), (1, 2)), ((), ())), preferred_element_type=jnp.float32
    )
    back = lax.ppermute(other_part.astype(jnp.bfloat16), "zlo", pair)
    sums = own_part + back.astype(jnp.float32)
    gate_sum = sums[:, :rows]
    up_sum = sums[:, rows:]
    hidden = (jax.nn.silu(gate_sum) * up_sum).astype(jnp.bfloat16)
    hidden_all, owners = ring_gather(hidden, ("zlo", "x"), narrow_count, narrow_index)
    down3 = jnp.take(down_block.reshape(narrow_count, rows, narrow_width), owners, axis=0, mode="clip")
    produced = lax.dot_general(
        hidden_all, down3, (((0, 2), (0, 1)), ((), ())), preferred_element_type=jnp.float32
    ).astype(jnp.bfloat16)

    produced, arrived = lax.optimization_barrier((produced, arrived))
    returned = lax.all_to_all(
        produced.reshape(groups, capacity, -1), "expert", split_axis=0, concat_axis=0, tiled=True
    ).reshape(groups * capacity, narrow_width)
    new_gate, new_up, new_down = unpack_weights(arrived, gate_block.shape, down_block.shape)
    layer_out = jnp.dot(combine, returned, preferred_element_type=jnp.float32).astype(jnp.bfloat16)
    return (
        layer_out,
        new_gate.reshape(gate_weight.shape),
        new_up.reshape(up_weight.shape),
        new_down.reshape(down_weight.shape),
    )


def solution(mesh):
    expert_size, narrow_size = mesh.devices.shape
    split_mesh = Mesh(
        mesh.devices.reshape(expert_size, 2, narrow_size // 2), ("expert", "zlo", "x")
    )
    narrow = ("zlo", "x")
    return jax.shard_map(
        body,
        mesh=split_mesh,
        in_specs=(
            P("expert", narrow),
            P("expert", None),
            P("expert", None),
            P(),
            P(),
            P("expert", narrow, None),
            P("expert", narrow, None),
            P("expert", None, narrow),
        ),
        out_specs=(
            P("expert", narrow),
            P("expert", narrow, None),
            P("expert", narrow, None),
            P("expert", None, narrow),
        ),
        check_vma=False,
    )
```

```python
import jax
import jax.numpy as jnp
from jax import lax
from jax.sharding import Mesh, PartitionSpec as P

LANES = 128


def slot_layout(route_ids, route_weight, holder, groups):
    tokens_here, top_count = route_ids.shape
    capacity = 2 * tokens_here * top_count // groups
    slot_ids = jnp.arange(groups, dtype=jnp.int32)
    matches = (holder[None, None, :] == route_ids[:, :, None]).astype(jnp.int32)
    target = jnp.sum(matches * slot_ids[None, None, :], axis=2)
    onehot = matches.reshape(tokens_here * top_count, groups)
    running = jnp.cumsum(onehot, axis=0) - 1
    position = jnp.sum(onehot * running, axis=1).reshape(tokens_here, top_count)
    row_index = target * capacity + position
    buffer_rows = jnp.arange(groups * capacity, dtype=jnp.int32)
    row_hits = buffer_rows[:, None, None] == row_index[None, :, :]
    dispatch = jnp.sum(row_hits.astype(jnp.float32), axis=2).astype(jnp.bfloat16)
    token_hits = row_index[:, :, None] == buffer_rows[None, None, :]
    combine = jnp.sum(
        jnp.where(token_hits, route_weight[:, :, None], jnp.zeros((), jnp.bfloat16)), axis=1
    )
    return (dispatch, combine, capacity)


def contract_last(left, right):
    return lax.dot_general(
        left, right, (((1,), (1,)), ((), ())), preferred_element_type=jnp.float32
    )


def pack_weights(gate, up, down, groups):
    rows, width = gate.shape
    depth, narrow_width = down.shape
    gate_c = gate.reshape(rows, width // LANES, LANES).transpose(1, 0, 2)
    up_c = up.reshape(rows, width // LANES, LANES).transpose(1, 0, 2)
    down_c = (
        down.reshape(depth // rows, rows, narrow_width // LANES, LANES)
        .transpose(0, 2, 1, 3)
        .reshape(-1, rows, LANES)
    )
    stacked = jnp.concatenate([gate_c, up_c, down_c], axis=0)
    return stacked.reshape(groups, -1, LANES)


def unpack_weights(packed, gate_shape, down_shape):
    rows, width = gate_shape
    depth, narrow_width = down_shape
    chunks = packed.reshape(-1, rows, LANES)
    n_gate = width // LANES
    gate = chunks[:n_gate].transpose(1, 0, 2).reshape(rows, width)
    up = chunks[n_gate : 2 * n_gate].transpose(1, 0, 2).reshape(rows, width)
    down = (
        chunks[2 * n_gate :]
        .reshape(depth // rows, narrow_width // LANES, rows, LANES)
        .transpose(0, 2, 1, 3)
        .reshape(depth, narrow_width)
    )
    return gate, up, down


def to_lanes(block, groups):
    return block.reshape(groups, -1, LANES)


def ring_gather(value, axis, size, index):
    pieces = [value]
    for shift in range(1, size):
        pieces.append(lax.ppermute(value, axis, [(i, (i + shift) % size) for i in range(size)]))
    sources = (index - jnp.arange(size, dtype=jnp.int32)) % size
    return jnp.stack(pieces, axis=0), sources


def body(tokens, route_ids, route_weight, partner, old_place, gate_weight, up_weight, down_weight):
    groups = lax.axis_size("expert")
    half = lax.axis_index("zlo")
    column = lax.axis_index("x")
    columns = lax.axis_size("x")
    narrow_count = lax.axis_size("zlo") * columns
    narrow_index = half * columns + column
    gate_block = gate_weight[0]
    up_block = up_weight[0]
    down_block = down_weight[0]
    rows, width = gate_block.shape
    depth, narrow_width = down_block.shape
    pair = [(0, 1), (1, 0)]

    gate_halves = gate_block.reshape(rows, 2, width // 2)
    up_halves = up_block.reshape(rows, 2, width // 2)
    keep = jnp.concatenate(
        [
            lax.dynamic_index_in_dim(gate_halves, half, axis=1, keepdims=False),
            lax.dynamic_index_in_dim(up_halves, half, axis=1, keepdims=False),
        ],
        axis=0,
    )
    give = jnp.concatenate(
        [
            lax.dynamic_index_in_dim(gate_halves, 1 - half, axis=1, keepdims=False),
            lax.dynamic_index_in_dim(up_halves, 1 - half, axis=1, keepdims=False),
        ],
        axis=0,
    )
    taken = lax.ppermute(give, "zlo", pair)

    dispatch, combine, capacity = slot_layout(route_ids, route_weight, old_place, groups)
    outgoing = jnp.dot(dispatch, tokens, preferred_element_type=jnp.float32).astype(jnp.bfloat16)
    packed = pack_weights(gate_block, up_block, down_block, groups)
    token_lanes = to_lanes(outgoing, groups)
    split_at = token_lanes.shape[1]
    first = lax.all_to_all(
        jnp.concatenate([token_lanes, packed], axis=1),
        "expert",
        split_axis=0,
        concat_axis=0,
        tiled=True,
    )
    slice_rows = first[:, :split_at].reshape(groups * capacity, narrow_width)
    spread = first[:, split_at:]
    ordered = jnp.take(spread, partner, axis=0, mode="clip")
    arrived = lax.all_to_all(ordered, "expert", split_axis=0, concat_axis=0, tiled=True)

    pieces, sources = ring_gather(slice_rows, "x", columns, column)
    keep3 = jnp.take(keep.reshape(keep.shape[0], columns, narrow_width), sources, axis=1, mode="clip")
    taken3 = jnp.take(
        taken.reshape(taken.shape[0], columns, narrow_width), sources, axis=1, mode="clip"
    )
    own_part = lax.dot_general(
        pieces, keep3, (((0, 2), (1, 2)), ((), ())), preferred_element_type=jnp.float32
    )
    other_part = lax.dot_general(
        pieces, taken3, (((0, 2), (1, 2)), ((), ())), preferred_element_type=jnp.float32
    )
    back = lax.ppermute(other_part, "zlo", pair)
    sums = own_part + back
    gate_sum = sums[:, :rows]
    up_sum = sums[:, rows:]
    hidden = (jax.nn.silu(gate_sum) * up_sum).astype(jnp.bfloat16)
    duo = jnp.stack([hidden, lax.ppermute(hidden, "zlo", pair)], axis=0)
    quads, sources = ring_gather(duo, "x", columns, column)
    hidden_all = quads.reshape(-1, hidden.shape[0], rows)
    owners = ((half + jnp.arange(2, dtype=jnp.int32)[None, :]) % 2) * columns + sources[:, None]
    down3 = jnp.take(
        down_block.reshape(narrow_count, rows, narrow_width), owners.reshape(-1), axis=0, mode="clip"
    )
    produced = lax.dot_general(
        hidden_all, down3, (((0, 2), (0, 1)), ((), ())), preferred_element_type=jnp.float32
    ).astype(jnp.bfloat16)

    produced, arrived = lax.optimization_barrier((produced, arrived))
    returned = lax.all_to_all(
        produced.reshape(groups, capacity, -1), "expert", split_axis=0, concat_axis=0, tiled=True
    ).reshape(groups * capacity, narrow_width)
    new_gate, new_up, new_down = unpack_weights(arrived, gate_block.shape, down_block.shape)
    layer_out = jnp.dot(combine, returned, preferred_element_type=jnp.float32).astype(jnp.bfloat16)
    return (
        layer_out,
        new_gate.reshape(gate_weight.shape),
        new_up.reshape(up_weight.shape),
        new_down.reshape(down_weight.shape),
    )


def solution(mesh):
    expert_size, narrow_size = mesh.devices.shape
    split_mesh = Mesh(
        mesh.devices.reshape(expert_size, 2, narrow_size // 2), ("expert", "zlo", "x")
    )
    narrow = ("zlo", "x")
    return jax.shard_map(
        body,
        mesh=split_mesh,
        in_specs=(
            P("expert", narrow),
            P("expert", None),
            P("expert", None),
            P(),
            P(),
            P("expert", narrow, None),
            P("expert", narrow, None),
            P("expert", None, narrow),
        ),
        out_specs=(
            P("expert", narrow),
            P("expert", narrow, None),
            P("expert", narrow, None),
            P("expert", None, narrow),
        ),
        check_vma=False,
    )
```

```python
import jax
import jax.numpy as jnp
from jax import lax
from jax.sharding import Mesh, PartitionSpec as P

LANES = 128


def slot_layout(route_ids, route_weight, holder, groups):
    tokens_here, top_count = route_ids.shape
    capacity = 2 * tokens_here * top_count // groups
    slot_ids = jnp.arange(groups, dtype=jnp.int32)
    matches = (holder[None, None, :] == route_ids[:, :, None]).astype(jnp.int32)
    target = jnp.sum(matches * slot_ids[None, None, :], axis=2)
    onehot = matches.reshape(tokens_here * top_count, groups)
    running = jnp.cumsum(onehot, axis=0) - 1
    position = jnp.sum(onehot * running, axis=1).reshape(tokens_here, top_count)
    row_index = target * capacity + position
    buffer_rows = jnp.arange(groups * capacity, dtype=jnp.int32)
    row_hits = buffer_rows[:, None, None] == row_index[None, :, :]
    dispatch = jnp.sum(row_hits.astype(jnp.float32), axis=2).astype(jnp.bfloat16)
    token_hits = row_index[:, :, None] == buffer_rows[None, None, :]
    combine = jnp.sum(
        jnp.where(token_hits, route_weight[:, :, None], jnp.zeros((), jnp.bfloat16)), axis=1
    )
    return (dispatch, combine, capacity)


def contract_last(left, right):
    return lax.dot_general(
        left, right, (((1,), (1,)), ((), ())), preferred_element_type=jnp.float32
    )


def pack_weights(gate, up, down, groups):
    rows, width = gate.shape
    depth, narrow_width = down.shape
    gate_c = gate.reshape(rows, width // LANES, LANES).transpose(1, 0, 2)
    up_c = up.reshape(rows, width // LANES, LANES).transpose(1, 0, 2)
    down_c = (
        down.reshape(depth // rows, rows, narrow_width // LANES, LANES)
        .transpose(0, 2, 1, 3)
        .reshape(-1, rows, LANES)
    )
    stacked = jnp.concatenate([gate_c, up_c, down_c], axis=0)
    return stacked.reshape(groups, -1, LANES)


def unpack_weights(packed, gate_shape, down_shape):
    rows, width = gate_shape
    depth, narrow_width = down_shape
    chunks = packed.reshape(-1, rows, LANES)
    n_gate = width // LANES
    gate = chunks[:n_gate].transpose(1, 0, 2).reshape(rows, width)
    up = chunks[n_gate : 2 * n_gate].transpose(1, 0, 2).reshape(rows, width)
    down = (
        chunks[2 * n_gate :]
        .reshape(depth // rows, narrow_width // LANES, rows, LANES)
        .transpose(0, 2, 1, 3)
        .reshape(depth, narrow_width)
    )
    return gate, up, down


def to_lanes(block, groups):
    return block.reshape(groups, -1, LANES)


def ring_gather(value, axis, size, index):
    pieces = [value]
    for shift in range(1, size):
        pieces.append(lax.ppermute(value, axis, [(i, (i + shift) % size) for i in range(size)]))
    sources = (index - jnp.arange(size, dtype=jnp.int32)) % size
    return jnp.stack(pieces, axis=0), sources


def body(tokens, route_ids, route_weight, partner, old_place, gate_weight, up_weight, down_weight):
    groups = lax.axis_size("expert")
    half = lax.axis_index("zlo")
    column = lax.axis_index("x")
    columns = lax.axis_size("x")
    halves = lax.axis_size("zlo")
    narrow_count = halves * columns
    narrow_index = half * columns + column
    gate_block = gate_weight[0]
    up_block = up_weight[0]
    down_block = down_weight[0]
    rows, width = gate_block.shape
    depth, narrow_width = down_block.shape
    pair = [(0, 1), (1, 0)]
    offsets = jnp.arange(columns, dtype=jnp.int32)

    both_weights = jnp.concatenate([gate_block, up_block], axis=0).reshape(
        2 * rows, narrow_count, narrow_width
    )
    weight_pieces = []
    for shift in range(columns):
        target = (column + shift) % columns
        wanted = jnp.stack([half * columns + target, (1 - half) * columns + target])
        piece = jnp.take(both_weights, wanted, axis=1, mode="clip").reshape(2 * rows, -1)
        if shift:
            piece = lax.ppermute(
                piece, "x", [(i, (i + shift) % columns) for i in range(columns)]
            )
        weight_pieces.append(piece)
    weights_here = jnp.stack(weight_pieces, axis=0)

    partner_tokens = lax.ppermute(tokens, "zlo", pair)
    wide_tokens = jnp.concatenate([tokens, partner_tokens], axis=1)

    dispatch, combine, capacity = slot_layout(route_ids, route_weight, old_place, groups)
    outgoing = jnp.dot(dispatch, wide_tokens, preferred_element_type=jnp.float32).astype(
        jnp.bfloat16
    )
    packed = pack_weights(gate_block, up_block, down_block, groups)
    token_lanes = to_lanes(outgoing, groups)
    split_at = token_lanes.shape[1]
    first = lax.all_to_all(
        jnp.concatenate([token_lanes, packed], axis=1),
        "expert",
        split_axis=0,
        concat_axis=0,
        tiled=True,
    )
    wide_rows = first[:, :split_at].reshape(groups * capacity, wide_tokens.shape[1])
    spread = first[:, split_at:]
    ordered = jnp.take(spread, partner, axis=0, mode="clip")
    arrived = lax.all_to_all(ordered, "expert", split_axis=0, concat_axis=0, tiled=True)

    parts = lax.dot_general(
        wide_rows, weights_here, (((1,), (2,)), ((), ())), preferred_element_type=jnp.float32
    )
    sums = parts[:, 0]
    for shift in range(1, columns):
        sums = sums + lax.ppermute(
            parts[:, shift], "x", [(i, (i - shift) % columns) for i in range(columns)]
        )
    gate_sum = sums[:, :rows]
    up_sum = sums[:, rows:]
    hidden = (jax.nn.silu(gate_sum) * up_sum).astype(jnp.bfloat16)
    hidden_all, owners = ring_gather(hidden, ("zlo", "x"), narrow_count, narrow_index)
    down3 = jnp.take(down_block.reshape(narrow_count, rows, narrow_width), owners, axis=0, mode="clip")
    produced = lax.dot_general(
        hidden_all, down3, (((0, 2), (0, 1)), ((), ())), preferred_element_type=jnp.float32
    ).astype(jnp.bfloat16)

    produced, arrived = lax.optimization_barrier((produced, arrived))
    returned = lax.all_to_all(
        produced.reshape(groups, capacity, -1), "expert", split_axis=0, concat_axis=0, tiled=True
    ).reshape(groups * capacity, narrow_width)
    new_gate, new_up, new_down = unpack_weights(arrived, gate_block.shape, down_block.shape)
    layer_out = jnp.dot(combine, returned, preferred_element_type=jnp.float32).astype(jnp.bfloat16)
    return (
        layer_out,
        new_gate.reshape(gate_weight.shape),
        new_up.reshape(up_weight.shape),
        new_down.reshape(down_weight.shape),
    )


def solution(mesh):
    expert_size, narrow_size = mesh.devices.shape
    split_mesh = Mesh(
        mesh.devices.reshape(expert_size, 2, narrow_size // 2), ("expert", "zlo", "x")
    )
    narrow = ("zlo", "x")
    return jax.shard_map(
        body,
        mesh=split_mesh,
        in_specs=(
            P("expert", narrow),
            P("expert", None),
            P("expert", None),
            P(),
            P(),
            P("expert", narrow, None),
            P("expert", narrow, None),
            P("expert", None, narrow),
        ),
        out_specs=(
            P("expert", narrow),
            P("expert", narrow, None),
            P("expert", narrow, None),
            P("expert", None, narrow),
        ),
        check_vma=False,
    )
```

```python
import jax
import jax.numpy as jnp
from jax import lax
from jax.sharding import Mesh, PartitionSpec as P

LANES = 128


def slot_layout(route_ids, route_weight, holder, groups):
    tokens_here, top_count = route_ids.shape
    capacity = 2 * tokens_here * top_count // groups
    slot_ids = jnp.arange(groups, dtype=jnp.int32)
    matches = (holder[None, None, :] == route_ids[:, :, None]).astype(jnp.int32)
    target = jnp.sum(matches * slot_ids[None, None, :], axis=2)
    onehot = matches.reshape(tokens_here * top_count, groups)
    running = jnp.cumsum(onehot, axis=0) - 1
    position = jnp.sum(onehot * running, axis=1).reshape(tokens_here, top_count)
    row_index = target * capacity + position
    buffer_rows = jnp.arange(groups * capacity, dtype=jnp.int32)
    row_hits = buffer_rows[:, None, None] == row_index[None, :, :]
    dispatch = jnp.sum(row_hits.astype(jnp.float32), axis=2).astype(jnp.bfloat16)
    token_hits = row_index[:, :, None] == buffer_rows[None, None, :]
    combine = jnp.sum(
        jnp.where(token_hits, route_weight[:, :, None], jnp.zeros((), jnp.bfloat16)), axis=1
    )
    return (dispatch, combine, capacity)


def contract_last(left, right):
    return lax.dot_general(
        left, right, (((1,), (1,)), ((), ())), preferred_element_type=jnp.float32
    )


def pack_weights(gate, up, down, groups):
    rows, width = gate.shape
    depth, narrow_width = down.shape
    gate_c = gate.reshape(rows, width // LANES, LANES).transpose(1, 0, 2)
    up_c = up.reshape(rows, width // LANES, LANES).transpose(1, 0, 2)
    down_c = (
        down.reshape(depth // rows, rows, narrow_width // LANES, LANES)
        .transpose(0, 2, 1, 3)
        .reshape(-1, rows, LANES)
    )
    stacked = jnp.concatenate([gate_c, up_c, down_c], axis=0)
    return stacked.reshape(groups, -1, LANES)


def unpack_weights(packed, gate_shape, down_shape):
    rows, width = gate_shape
    depth, narrow_width = down_shape
    chunks = packed.reshape(-1, rows, LANES)
    n_gate = width // LANES
    gate = chunks[:n_gate].transpose(1, 0, 2).reshape(rows, width)
    up = chunks[n_gate : 2 * n_gate].transpose(1, 0, 2).reshape(rows, width)
    down = (
        chunks[2 * n_gate :]
        .reshape(depth // rows, narrow_width // LANES, rows, LANES)
        .transpose(0, 2, 1, 3)
        .reshape(depth, narrow_width)
    )
    return gate, up, down


def to_lanes(block, groups):
    return block.reshape(groups, -1, LANES)


def ring_gather(value, axis, size, index):
    pieces = [value]
    for shift in range(1, size):
        pieces.append(lax.ppermute(value, axis, [(i, (i + shift) % size) for i in range(size)]))
    sources = (index - jnp.arange(size, dtype=jnp.int32)) % size
    return jnp.stack(pieces, axis=0), sources


def body(tokens, route_ids, route_weight, partner, old_place, gate_weight, up_weight, down_weight):
    groups = lax.axis_size("expert")
    half = lax.axis_index("zlo")
    column = lax.axis_index("x")
    columns = lax.axis_size("x")
    narrow_count = lax.axis_size("zlo") * columns
    narrow_index = half * columns + column
    gate_block = gate_weight[0]
    up_block = up_weight[0]
    down_block = down_weight[0]
    rows, width = gate_block.shape
    depth, narrow_width = down_block.shape
    pair = [(0, 1), (1, 0)]

    gate_halves = gate_block.reshape(rows, 2, width // 2)
    up_halves = up_block.reshape(rows, 2, width // 2)
    keep = jnp.concatenate(
        [
            lax.dynamic_index_in_dim(gate_halves, half, axis=1, keepdims=False),
            lax.dynamic_index_in_dim(up_halves, half, axis=1, keepdims=False),
        ],
        axis=0,
    )
    give = jnp.concatenate(
        [
            lax.dynamic_index_in_dim(gate_halves, 1 - half, axis=1, keepdims=False),
            lax.dynamic_index_in_dim(up_halves, 1 - half, axis=1, keepdims=False),
        ],
        axis=0,
    )
    taken = lax.ppermute(give, "zlo", pair)

    dispatch, combine, capacity = slot_layout(route_ids, route_weight, old_place, groups)
    outgoing = jnp.dot(dispatch, tokens, preferred_element_type=jnp.float32).astype(jnp.bfloat16)
    packed = pack_weights(gate_block, up_block, down_block, groups)
    token_lanes = to_lanes(outgoing, groups)
    split_at = token_lanes.shape[1]
    room = jnp.concatenate(
        [jnp.zeros(token_lanes.shape, token_lanes.dtype), packed], axis=1
    )
    first = lax.all_to_all(
        lax.dynamic_update_slice_in_dim(room, token_lanes, 0, axis=1),
        "expert",
        split_axis=0,
        concat_axis=0,
        tiled=True,
    )
    slice_rows = first[:, :split_at].reshape(groups * capacity, narrow_width)
    spread = first[:, split_at:]
    ordered = jnp.take(spread, partner, axis=0, mode="clip")
    arrived = lax.all_to_all(ordered, "expert", split_axis=0, concat_axis=0, tiled=True)

    sources = (column - jnp.arange(columns, dtype=jnp.int32)) % columns
    keep3 = jnp.take(keep.reshape(keep.shape[0], columns, narrow_width), sources, axis=1, mode="clip")
    taken3 = jnp.take(
        taken.reshape(taken.shape[0], columns, narrow_width), sources, axis=1, mode="clip"
    )
    keep3, taken3, slice_rows, spread = lax.optimization_barrier((keep3, taken3, slice_rows, spread))
    pieces, sources = ring_gather(slice_rows, "x", columns, column)
    own_part = lax.dot_general(
        pieces, keep3, (((0, 2), (1, 2)), ((), ())), preferred_element_type=jnp.float32
    )
    other_part = lax.dot_general(
        pieces, taken3, (((0, 2), (1, 2)), ((), ())), preferred_element_type=jnp.float32
    )
    back = lax.ppermute(other_part, "zlo", pair)
    sums = own_part + back
    gate_sum = sums[:, :rows]
    up_sum = sums[:, rows:]
    hidden = (jax.nn.silu(gate_sum) * up_sum).astype(jnp.bfloat16)
    hidden_all, owners = ring_gather(hidden, ("zlo", "x"), narrow_count, narrow_index)
    down3 = jnp.take(down_block.reshape(narrow_count, rows, narrow_width), owners, axis=0, mode="clip")
    produced = lax.dot_general(
        hidden_all, down3, (((0, 2), (0, 1)), ((), ())), preferred_element_type=jnp.float32
    ).astype(jnp.bfloat16)

    produced, arrived = lax.optimization_barrier((produced, arrived))
    returned = lax.all_to_all(
        produced.reshape(groups, capacity, -1), "expert", split_axis=0, concat_axis=0, tiled=True
    ).reshape(groups * capacity, narrow_width)
    new_gate, new_up, new_down = unpack_weights(arrived, gate_block.shape, down_block.shape)
    layer_out = jnp.dot(combine, returned, preferred_element_type=jnp.float32).astype(jnp.bfloat16)
    return (
        layer_out,
        new_gate.reshape(gate_weight.shape),
        new_up.reshape(up_weight.shape),
        new_down.reshape(down_weight.shape),
    )


def solution(mesh):
    expert_size, narrow_size = mesh.devices.shape
    split_mesh = Mesh(
        mesh.devices.reshape(expert_size, 2, narrow_size // 2), ("expert", "zlo", "x")
    )
    narrow = ("zlo", "x")
    return jax.shard_map(
        body,
        mesh=split_mesh,
        in_specs=(
            P("expert", narrow),
            P("expert", None),
            P("expert", None),
            P(),
            P(),
            P("expert", narrow, None),
            P("expert", narrow, None),
            P("expert", None, narrow),
        ),
        out_specs=(
            P("expert", narrow),
            P("expert", narrow, None),
            P("expert", narrow, None),
            P("expert", None, narrow),
        ),
        check_vma=False,
    )
```

```python
import jax
import jax.numpy as jnp
from jax import lax
from jax.sharding import Mesh, PartitionSpec as P

LANES = 128


def slot_layout(route_ids, route_weight, holder, groups):
    tokens_here, top_count = route_ids.shape
    capacity = 2 * tokens_here * top_count // groups
    slot_ids = jnp.arange(groups, dtype=jnp.int32)
    matches = (holder[None, None, :] == route_ids[:, :, None]).astype(jnp.int32)
    target = jnp.sum(matches * slot_ids[None, None, :], axis=2)
    onehot = matches.reshape(tokens_here * top_count, groups)
    running = jnp.cumsum(onehot, axis=0) - 1
    position = jnp.sum(onehot * running, axis=1).reshape(tokens_here, top_count)
    row_index = target * capacity + position
    buffer_rows = jnp.arange(groups * capacity, dtype=jnp.int32)
    row_hits = buffer_rows[:, None, None] == row_index[None, :, :]
    dispatch = jnp.sum(row_hits.astype(jnp.float32), axis=2).astype(jnp.bfloat16)
    token_hits = row_index[:, :, None] == buffer_rows[None, None, :]
    combine = jnp.sum(
        jnp.where(token_hits, route_weight[:, :, None], jnp.zeros((), jnp.bfloat16)), axis=1
    )
    return (dispatch, combine, capacity)


def contract_last(left, right):
    return lax.dot_general(
        left, right, (((1,), (1,)), ((), ())), preferred_element_type=jnp.float32
    )


def pack_weights(gate, up, down, groups):
    rows, width = gate.shape
    depth, narrow_width = down.shape
    gate_c = gate.reshape(rows, width // LANES, LANES).transpose(1, 0, 2)
    up_c = up.reshape(rows, width // LANES, LANES).transpose(1, 0, 2)
    down_c = (
        down.reshape(depth // rows, rows, narrow_width // LANES, LANES)
        .transpose(0, 2, 1, 3)
        .reshape(-1, rows, LANES)
    )
    stacked = jnp.concatenate([gate_c, up_c, down_c], axis=0)
    return stacked.reshape(groups, -1, LANES)


def unpack_weights(packed, gate_shape, down_shape):
    rows, width = gate_shape
    depth, narrow_width = down_shape
    chunks = packed.reshape(-1, rows, LANES)
    n_gate = width // LANES
    gate = chunks[:n_gate].transpose(1, 0, 2).reshape(rows, width)
    up = chunks[n_gate : 2 * n_gate].transpose(1, 0, 2).reshape(rows, width)
    down = (
        chunks[2 * n_gate :]
        .reshape(depth // rows, narrow_width // LANES, rows, LANES)
        .transpose(0, 2, 1, 3)
        .reshape(depth, narrow_width)
    )
    return gate, up, down


def to_lanes(block, groups):
    return block.reshape(groups, -1, LANES)


def ring_gather(value, axis, size, index):
    pieces = [value]
    for shift in range(1, size):
        pieces.append(lax.ppermute(value, axis, [(i, (i + shift) % size) for i in range(size)]))
    sources = (index - jnp.arange(size, dtype=jnp.int32)) % size
    return jnp.stack(pieces, axis=0), sources


def body(tokens, route_ids, route_weight, partner, old_place, gate_weight, up_weight, down_weight):
    groups = lax.axis_size("expert")
    half = lax.axis_index("zlo")
    column = lax.axis_index("x")
    columns = lax.axis_size("x")
    narrow_count = lax.axis_size("zlo") * columns
    narrow_index = half * columns + column
    gate_block = gate_weight[0]
    up_block = up_weight[0]
    down_block = down_weight[0]
    rows, width = gate_block.shape
    depth, narrow_width = down_block.shape
    pair = [(0, 1), (1, 0)]

    gate_halves = gate_block.reshape(rows, 2, width // 2)
    up_halves = up_block.reshape(rows, 2, width // 2)
    keep = jnp.concatenate(
        [
            lax.dynamic_index_in_dim(gate_halves, half, axis=1, keepdims=False),
            lax.dynamic_index_in_dim(up_halves, half, axis=1, keepdims=False),
        ],
        axis=0,
    )
    give = jnp.concatenate(
        [
            lax.dynamic_index_in_dim(gate_halves, 1 - half, axis=1, keepdims=False),
            lax.dynamic_index_in_dim(up_halves, 1 - half, axis=1, keepdims=False),
        ],
        axis=0,
    )
    taken = lax.ppermute(give, "zlo", pair)

    dispatch, combine, capacity = slot_layout(route_ids, route_weight, old_place, groups)
    outgoing = jnp.dot(dispatch, tokens, preferred_element_type=jnp.float32).astype(jnp.bfloat16)
    packed = pack_weights(gate_block, up_block, down_block, groups)
    token_lanes = to_lanes(outgoing, groups)
    split_at = token_lanes.shape[1]
    first = lax.all_to_all(
        jnp.concatenate([token_lanes, packed], axis=1),
        "expert",
        split_axis=0,
        concat_axis=0,
        tiled=True,
    )
    slice_rows = first[:, :split_at].reshape(groups * capacity, narrow_width)
    spread = first[:, split_at:]
    ordered = jnp.take(spread, partner, axis=0, mode="clip")
    ordered, slice_rows = lax.optimization_barrier((ordered, slice_rows))
    arrived = lax.all_to_all(ordered, "expert", split_axis=0, concat_axis=0, tiled=True)

    pieces, sources = ring_gather(slice_rows, "x", columns, column)
    keep3 = jnp.take(keep.reshape(keep.shape[0], columns, narrow_width), sources, axis=1, mode="clip")
    taken3 = jnp.take(
        taken.reshape(taken.shape[0], columns, narrow_width), sources, axis=1, mode="clip"
    )
    own_part = lax.dot_general(
        pieces, keep3, (((0, 2), (1, 2)), ((), ())), preferred_element_type=jnp.float32
    )
    other_part = lax.dot_general(
        pieces, taken3, (((0, 2), (1, 2)), ((), ())), preferred_element_type=jnp.float32
    )
    back = lax.ppermute(other_part, "zlo", pair)
    sums = own_part + back
    gate_sum = sums[:, :rows]
    up_sum = sums[:, rows:]
    hidden = (jax.nn.silu(gate_sum) * up_sum).astype(jnp.bfloat16)
    hidden_all, owners = ring_gather(hidden, ("zlo", "x"), narrow_count, narrow_index)
    down3 = jnp.take(down_block.reshape(narrow_count, rows, narrow_width), owners, axis=0, mode="clip")
    produced = lax.dot_general(
        hidden_all, down3, (((0, 2), (0, 1)), ((), ())), preferred_element_type=jnp.float32
    ).astype(jnp.bfloat16)

    produced, arrived = lax.optimization_barrier((produced, arrived))
    returned = lax.all_to_all(
        produced.reshape(groups, capacity, -1), "expert", split_axis=0, concat_axis=0, tiled=True
    ).reshape(groups * capacity, narrow_width)
    new_gate, new_up, new_down = unpack_weights(arrived, gate_block.shape, down_block.shape)
    layer_out = jnp.dot(combine, returned, preferred_element_type=jnp.float32).astype(jnp.bfloat16)
    return (
        layer_out,
        new_gate.reshape(gate_weight.shape),
        new_up.reshape(up_weight.shape),
        new_down.reshape(down_weight.shape),
    )


def solution(mesh):
    expert_size, narrow_size = mesh.devices.shape
    split_mesh = Mesh(
        mesh.devices.reshape(expert_size, 2, narrow_size // 2), ("expert", "zlo", "x")
    )
    narrow = ("zlo", "x")
    return jax.shard_map(
        body,
        mesh=split_mesh,
        in_specs=(
            P("expert", narrow),
            P("expert", None),
            P("expert", None),
            P(),
            P(),
            P("expert", narrow, None),
            P("expert", narrow, None),
            P("expert", None, narrow),
        ),
        out_specs=(
            P("expert", narrow),
            P("expert", narrow, None),
            P("expert", narrow, None),
            P("expert", None, narrow),
        ),
        check_vma=False,
    )
```

```python
import jax
import jax.numpy as jnp
from jax import lax
from jax.sharding import Mesh, PartitionSpec as P

LANES = 128


def slot_layout(route_ids, route_weight, holder, groups):
    tokens_here, top_count = route_ids.shape
    capacity = 2 * tokens_here * top_count // groups
    slot_ids = jnp.arange(groups, dtype=jnp.int32)
    matches = (holder[None, None, :] == route_ids[:, :, None]).astype(jnp.int32)
    target = jnp.sum(matches * slot_ids[None, None, :], axis=2)
    onehot = matches.reshape(tokens_here * top_count, groups)
    running = jnp.cumsum(onehot, axis=0) - 1
    position = jnp.sum(onehot * running, axis=1).reshape(tokens_here, top_count)
    row_index = target * capacity + position
    buffer_rows = jnp.arange(groups * capacity, dtype=jnp.int32)
    row_hits = buffer_rows[:, None, None] == row_index[None, :, :]
    dispatch = jnp.sum(row_hits.astype(jnp.float32), axis=2).astype(jnp.bfloat16)
    token_hits = row_index[:, :, None] == buffer_rows[None, None, :]
    combine = jnp.sum(
        jnp.where(token_hits, route_weight[:, :, None], jnp.zeros((), jnp.bfloat16)), axis=1
    )
    return (dispatch, combine, capacity)


def contract_last(left, right):
    return lax.dot_general(
        left, right, (((1,), (1,)), ((), ())), preferred_element_type=jnp.float32
    )


def pack_weights(gate, up, down, groups):
    rows, width = gate.shape
    depth, narrow_width = down.shape
    gate_c = gate.reshape(rows, width // LANES, LANES).transpose(1, 0, 2)
    up_c = up.reshape(rows, width // LANES, LANES).transpose(1, 0, 2)
    down_c = (
        down.reshape(depth // rows, rows, narrow_width // LANES, LANES)
        .transpose(0, 2, 1, 3)
        .reshape(-1, rows, LANES)
    )
    pair_c = jnp.concatenate([gate_c, up_c], axis=0)
    return pair_c.reshape(groups, -1, LANES), down_c.reshape(groups, -1, LANES)


def unpack_weights(pair_packed, down_packed, gate_shape, down_shape):
    rows, width = gate_shape
    depth, narrow_width = down_shape
    chunks = pair_packed.reshape(-1, rows, LANES)
    n_gate = width // LANES
    gate = chunks[:n_gate].transpose(1, 0, 2).reshape(rows, width)
    up = chunks[n_gate:].transpose(1, 0, 2).reshape(rows, width)
    down = (
        down_packed.reshape(depth // rows, narrow_width // LANES, rows, LANES)
        .transpose(0, 2, 1, 3)
        .reshape(depth, narrow_width)
    )
    return gate, up, down


def to_lanes(block, groups):
    return block.reshape(groups, -1, LANES)


def ring_gather(value, axis, size, index):
    pieces = [value]
    for shift in range(1, size):
        pieces.append(lax.ppermute(value, axis, [(i, (i + shift) % size) for i in range(size)]))
    sources = (index - jnp.arange(size, dtype=jnp.int32)) % size
    return jnp.stack(pieces, axis=0), sources


def body(tokens, route_ids, route_weight, partner, old_place, gate_weight, up_weight, down_weight):
    groups = lax.axis_size("expert")
    half = lax.axis_index("zlo")
    column = lax.axis_index("x")
    columns = lax.axis_size("x")
    narrow_count = lax.axis_size("zlo") * columns
    narrow_index = half * columns + column
    gate_block = gate_weight[0]
    up_block = up_weight[0]
    down_block = down_weight[0]
    rows, width = gate_block.shape
    depth, narrow_width = down_block.shape
    pair = [(0, 1), (1, 0)]

    gate_halves = gate_block.reshape(rows, 2, width // 2)
    up_halves = up_block.reshape(rows, 2, width // 2)
    keep = jnp.concatenate(
        [
            lax.dynamic_index_in_dim(gate_halves, half, axis=1, keepdims=False),
            lax.dynamic_index_in_dim(up_halves, half, axis=1, keepdims=False),
        ],
        axis=0,
    )
    give = jnp.concatenate(
        [
            lax.dynamic_index_in_dim(gate_halves, 1 - half, axis=1, keepdims=False),
            lax.dynamic_index_in_dim(up_halves, 1 - half, axis=1, keepdims=False),
        ],
        axis=0,
    )
    taken = lax.ppermute(give, "zlo", pair)

    dispatch, combine, capacity = slot_layout(route_ids, route_weight, old_place, groups)
    outgoing = jnp.dot(dispatch, tokens, preferred_element_type=jnp.float32).astype(jnp.bfloat16)
    pair_packed, down_packed = pack_weights(gate_block, up_block, down_block, groups)
    token_lanes = to_lanes(outgoing, groups)
    split_at = token_lanes.shape[1]
    pair_at = split_at + pair_packed.shape[1]
    first = lax.all_to_all(
        jnp.concatenate([token_lanes, pair_packed, down_packed], axis=1),
        "expert",
        split_axis=0,
        concat_axis=0,
        tiled=True,
    )
    slice_rows = first[:, :split_at].reshape(groups * capacity, narrow_width)
    pair_spread = first[:, split_at:pair_at]
    down_spread = first[:, pair_at:]
    pair_ordered = jnp.take(pair_spread, partner, axis=0, mode="clip")
    arrived = lax.all_to_all(pair_ordered, "expert", split_axis=0, concat_axis=0, tiled=True)

    pieces, sources = ring_gather(slice_rows, "x", columns, column)
    keep3 = jnp.take(keep.reshape(keep.shape[0], columns, narrow_width), sources, axis=1, mode="clip")
    taken3 = jnp.take(
        taken.reshape(taken.shape[0], columns, narrow_width), sources, axis=1, mode="clip"
    )
    own_part = lax.dot_general(
        pieces, keep3, (((0, 2), (1, 2)), ((), ())), preferred_element_type=jnp.float32
    )
    other_part = lax.dot_general(
        pieces, taken3, (((0, 2), (1, 2)), ((), ())), preferred_element_type=jnp.float32
    )
    back = lax.ppermute(other_part, "zlo", pair)
    sums = own_part + back
    gate_sum = sums[:, :rows]
    up_sum = sums[:, rows:]
    hidden = (jax.nn.silu(gate_sum) * up_sum).astype(jnp.bfloat16)
    hidden_all, owners = ring_gather(hidden, ("zlo", "x"), narrow_count, narrow_index)
    down3 = jnp.take(down_block.reshape(narrow_count, rows, narrow_width), owners, axis=0, mode="clip")
    produced = lax.dot_general(
        hidden_all, down3, (((0, 2), (0, 1)), ((), ())), preferred_element_type=jnp.float32
    ).astype(jnp.bfloat16)

    produced, arrived = lax.optimization_barrier((produced, arrived))
    down_ordered = jnp.take(down_spread, partner, axis=0, mode="clip")
    second = lax.all_to_all(
        jnp.concatenate([to_lanes(produced, groups), down_ordered], axis=1),
        "expert",
        split_axis=0,
        concat_axis=0,
        tiled=True,
    )
    returned = second[:, :split_at].reshape(groups * capacity, narrow_width)
    new_gate, new_up, new_down = unpack_weights(
        arrived, second[:, split_at:], gate_block.shape, down_block.shape
    )
    layer_out = jnp.dot(combine, returned, preferred_element_type=jnp.float32).astype(jnp.bfloat16)
    return (
        layer_out,
        new_gate.reshape(gate_weight.shape),
        new_up.reshape(up_weight.shape),
        new_down.reshape(down_weight.shape),
    )


def solution(mesh):
    expert_size, narrow_size = mesh.devices.shape
    split_mesh = Mesh(
        mesh.devices.reshape(expert_size, 2, narrow_size // 2), ("expert", "zlo", "x")
    )
    narrow = ("zlo", "x")
    return jax.shard_map(
        body,
        mesh=split_mesh,
        in_specs=(
            P("expert", narrow),
            P("expert", None),
            P("expert", None),
            P(),
            P(),
            P("expert", narrow, None),
            P("expert", narrow, None),
            P("expert", None, narrow),
        ),
        out_specs=(
            P("expert", narrow),
            P("expert", narrow, None),
            P("expert", narrow, None),
            P("expert", None, narrow),
        ),
        check_vma=False,
    )
```

```python
import jax
import jax.numpy as jnp
from jax import lax
from jax.sharding import Mesh, PartitionSpec as P

LANES = 128


def slot_layout(route_ids, route_weight, holder, groups):
    tokens_here, top_count = route_ids.shape
    capacity = 2 * tokens_here * top_count // groups
    slot_ids = jnp.arange(groups, dtype=jnp.int32)
    matches = (holder[None, None, :] == route_ids[:, :, None]).astype(jnp.int32)
    target = jnp.sum(matches * slot_ids[None, None, :], axis=2)
    onehot = matches.reshape(tokens_here * top_count, groups)
    running = jnp.cumsum(onehot, axis=0) - 1
    position = jnp.sum(onehot * running, axis=1).reshape(tokens_here, top_count)
    row_index = target * capacity + position
    buffer_rows = jnp.arange(groups * capacity, dtype=jnp.int32)
    row_hits = buffer_rows[:, None, None] == row_index[None, :, :]
    dispatch = jnp.sum(row_hits.astype(jnp.float32), axis=2).astype(jnp.bfloat16)
    token_hits = row_index[:, :, None] == buffer_rows[None, None, :]
    combine = jnp.sum(
        jnp.where(token_hits, route_weight[:, :, None], jnp.zeros((), jnp.bfloat16)), axis=1
    )
    return (dispatch, combine, capacity)


def contract_last(left, right):
    return lax.dot_general(
        left, right, (((1,), (1,)), ((), ())), preferred_element_type=jnp.float32
    )


def pack_weights(gate, up, down, groups):
    rows, width = gate.shape
    depth, narrow_width = down.shape
    gate_c = gate.reshape(rows, width // LANES, LANES).transpose(1, 0, 2)
    up_c = up.reshape(rows, width // LANES, LANES).transpose(1, 0, 2)
    down_c = (
        down.reshape(depth // rows, rows, narrow_width // LANES, LANES)
        .transpose(0, 2, 1, 3)
        .reshape(-1, rows, LANES)
    )
    stacked = jnp.concatenate([gate_c, up_c, down_c], axis=0)
    return stacked.reshape(groups, -1, LANES)


def unpack_weights(packed, gate_shape, down_shape):
    rows, width = gate_shape
    depth, narrow_width = down_shape
    chunks = packed.reshape(-1, rows, LANES)
    n_gate = width // LANES
    gate = chunks[:n_gate].transpose(1, 0, 2).reshape(rows, width)
    up = chunks[n_gate : 2 * n_gate].transpose(1, 0, 2).reshape(rows, width)
    down = (
        chunks[2 * n_gate :]
        .reshape(depth // rows, narrow_width // LANES, rows, LANES)
        .transpose(0, 2, 1, 3)
        .reshape(depth, narrow_width)
    )
    return gate, up, down


def to_lanes(block, groups):
    return block.reshape(groups, -1, LANES)


def ring_gather(value, axis, size, index):
    pieces = [value]
    for shift in range(1, size):
        pieces.append(lax.ppermute(value, axis, [(i, (i + shift) % size) for i in range(size)]))
    sources = (index - jnp.arange(size, dtype=jnp.int32)) % size
    return jnp.stack(pieces, axis=0), sources


def body(tokens, route_ids, route_weight, partner, old_place, gate_weight, up_weight, down_weight):
    groups = lax.axis_size("expert")
    half = lax.axis_index("zlo")
    column = lax.axis_index("x")
    columns = lax.axis_size("x")
    narrow_count = lax.axis_size("zlo") * columns
    narrow_index = half * columns + column
    gate_block = gate_weight[0]
    up_block = up_weight[0]
    down_block = down_weight[0]
    rows, width = gate_block.shape
    depth, narrow_width = down_block.shape
    pair = [(0, 1), (1, 0)]

    gate_halves = gate_block.reshape(rows, 2, width // 2)
    up_halves = up_block.reshape(rows, 2, width // 2)
    keep = jnp.concatenate(
        [
            lax.dynamic_index_in_dim(gate_halves, half, axis=1, keepdims=False),
            lax.dynamic_index_in_dim(up_halves, half, axis=1, keepdims=False),
        ],
        axis=0,
    )
    give = jnp.concatenate(
        [
            lax.dynamic_index_in_dim(gate_halves, 1 - half, axis=1, keepdims=False),
            lax.dynamic_index_in_dim(up_halves, 1 - half, axis=1, keepdims=False),
        ],
        axis=0,
    )
    taken = lax.ppermute(give, "zlo", pair)

    dispatch, combine, capacity = slot_layout(route_ids, route_weight, old_place, groups)
    outgoing = jnp.dot(dispatch, tokens, preferred_element_type=jnp.float32).astype(jnp.bfloat16)
    packed = pack_weights(gate_block, up_block, down_block, groups)
    token_lanes = to_lanes(outgoing, groups)
    split_at = token_lanes.shape[1]
    first = lax.all_to_all(
        jnp.concatenate([token_lanes, packed], axis=1),
        "expert",
        split_axis=0,
        concat_axis=0,
        tiled=True,
    )
    slice_rows = first[:, :split_at].reshape(groups * capacity, narrow_width)
    spread = first[:, split_at:]
    ordered = jnp.take(spread, partner, axis=0, mode="clip")
    arrived = lax.all_to_all(ordered, "expert", split_axis=0, concat_axis=0, tiled=True)

    pieces, sources = ring_gather(slice_rows, "x", columns, column)
    keep3 = jnp.take(keep.reshape(keep.shape[0], columns, narrow_width), sources, axis=1, mode="clip")
    taken3 = jnp.take(
        taken.reshape(taken.shape[0], columns, narrow_width), sources, axis=1, mode="clip"
    )
    other_part = lax.dot_general(
        pieces, taken3, (((0, 2), (1, 2)), ((), ())), preferred_element_type=jnp.float32
    )
    back = lax.ppermute(other_part, "zlo", pair)
    pieces, keep3, other_part = lax.optimization_barrier((pieces, keep3, other_part))
    own_part = lax.dot_general(
        pieces, keep3, (((0, 2), (1, 2)), ((), ())), preferred_element_type=jnp.float32
    )
    sums = own_part + back
    gate_sum = sums[:, :rows]
    up_sum = sums[:, rows:]
    hidden = (jax.nn.silu(gate_sum) * up_sum).astype(jnp.bfloat16)
    hidden_all, owners = ring_gather(hidden, ("zlo", "x"), narrow_count, narrow_index)
    down3 = jnp.take(down_block.reshape(narrow_count, rows, narrow_width), owners, axis=0, mode="clip")
    produced = lax.dot_general(
        hidden_all, down3, (((0, 2), (0, 1)), ((), ())), preferred_element_type=jnp.float32
    ).astype(jnp.bfloat16)

    produced, arrived = lax.optimization_barrier((produced, arrived))
    returned = lax.all_to_all(
        produced.reshape(groups, capacity, -1), "expert", split_axis=0, concat_axis=0, tiled=True
    ).reshape(groups * capacity, narrow_width)
    new_gate, new_up, new_down = unpack_weights(arrived, gate_block.shape, down_block.shape)
    layer_out = jnp.dot(combine, returned, preferred_element_type=jnp.float32).astype(jnp.bfloat16)
    return (
        layer_out,
        new_gate.reshape(gate_weight.shape),
        new_up.reshape(up_weight.shape),
        new_down.reshape(down_weight.shape),
    )


def solution(mesh):
    expert_size, narrow_size = mesh.devices.shape
    split_mesh = Mesh(
        mesh.devices.reshape(expert_size, 2, narrow_size // 2), ("expert", "zlo", "x")
    )
    narrow = ("zlo", "x")
    return jax.shard_map(
        body,
        mesh=split_mesh,
        in_specs=(
            P("expert", narrow),
            P("expert", None),
            P("expert", None),
            P(),
            P(),
            P("expert", narrow, None),
            P("expert", narrow, None),
            P("expert", None, narrow),
        ),
        out_specs=(
            P("expert", narrow),
            P("expert", narrow, None),
            P("expert", narrow, None),
            P("expert", None, narrow),
        ),
        check_vma=False,
    )
```
